32 devices in a mesh: depth: 4 (over z), region: 8 (over y, x, core).
Axes of the slice: x: 2, y: 2, z: 4, core: 2. Of those that a mesh axis runs over, the one named last changes fastest.
Arguments:
- thermal_grid: float32 [8, 128, 4096], P('depth', None, 'region'), may hold values from -6 to 6
- colormap_samples: float32 [4, 256], replicated, may hold values from 0.05 to 1
- sheetgroup_viewer_sequence: int32 [4], replicated, may hold values from 0 to 3, each once
- occupied_lines: int32 [4, 8], P('depth', 'region'), may hold values from 64 to 128
- skew_offsets: int32 [1], replicated, may hold values from 256 to 511
Outputs:
- image: float32 [4, 128, 4096], P(None, 'depth', 'region')
The draws below stay inside these ranges and needn't reach their ends.
Inputs may be any that keep to these rules, and one draw needn't show every extreme that they name: `sheetgroup_viewer_sequence`: each rank appears once.
All inputs are finite; a program needn't handle non-finite values.
Results may differ from the reference program's by a relative error of at most 0.0003.
Values sent between devices are 32-bit elements; how exact they have to be, the bound alone decides.
No kernel may reach another device: no remote copies, remote signals or barrier semaphores. Data moves between devices by JAX's collectives and lax.ppermute only.
A program may use at most 64 MiB of HBM per device.

```python
import jax
import jax.numpy as jnp
from jax import lax

PIECE_SHEETS = 2
PIECE_LINES = 128
BX = 512
KNOTS = 256
SHEET_COUNT = 8
GRID_WIDTH = 4096
N_DEPTH = 4
N_REGION = 8


def with_ends(result, rng, smallest, largest):
    place = [jax.random.randint(jax.random.fold_in(rng, axis), (), 0, length) for axis, length in enumerate(result.shape)]
    main_axis = result.shape.index(max(result.shape))
    next_to = place[:main_axis] + [(place[main_axis] + 1) % result.shape[main_axis]] + place[main_axis + 1:]
    return result.at[tuple(place)].set(smallest).at[tuple(next_to)].set(largest)


def level_of(stream_key, shape, pieces, low, top_value):
    gain, own = 1.0, jax.random.fold_in(stream_key, 6)
    for dim, shards_of in pieces:
        draws = jnp.exp(jax.random.uniform(jax.random.fold_in(own, dim), (shards_of,), jnp.float32, low / len(pieces), top_value / len(pieces)))
        gain = gain * jnp.repeat(draws, shape[dim] // shards_of).reshape([-1 if axis == dim else 1 for axis in range(len(shape))])
    return gain


def centred(own_key, shape, scale, bound, pieces=(), held_as=jnp.bfloat16):
    values = jax.random.normal(own_key, shape, jnp.float32) * scale
    if len(pieces) > 0:
        values = level_of(own_key, shape, pieces, -0.22, 0.18) * values
    return jnp.clip(values, min=-bound, max=bound).astype(held_as)


def setup_inputs(seed: int = 0) -> dict:
    splits = jax.random.split(jax.random.key(seed), 6)
    thermal_grid = centred(splits[0], (SHEET_COUNT, PIECE_LINES, GRID_WIDTH), 1.0, 6.0, ((0, 4), (2, 8)), jnp.float32)
    colormap_samples = jnp.clip(jax.random.uniform(splits[1], (4, KNOTS), jnp.float32, 0.05, 1.0), 0.05, 1.0)
    sheetgroup_viewer_sequence = jax.random.permutation(splits[2], N_DEPTH).astype(jnp.int32)
    occupied_lines = with_ends(jax.random.randint(splits[3], (N_DEPTH, N_REGION), PIECE_LINES // 2, PIECE_LINES + 1), jax.random.fold_in(splits[3], 1), PIECE_LINES // 2, PIECE_LINES).astype(jnp.int32)
    skew_offsets = jax.random.randint(splits[4], (1,), BX // 2, BX).astype(jnp.int32)
    return dict(thermal_grid=thermal_grid, colormap_samples=colormap_samples, sheetgroup_viewer_sequence=sheetgroup_viewer_sequence, occupied_lines=occupied_lines, skew_offsets=skew_offsets)


def transfer(cells, colormap_samples):
    scaled = jnp.clip((cells + 3.0) * ((KNOTS - 1) / 6.0), 0.0, KNOTS - 1.0)
    lower = jnp.minimum(jnp.floor(scaled), KNOTS - 2.0)
    fraction = scaled - lower
    index = lower.astype(jnp.int32)
    low_value = jnp.take(colormap_samples, index, axis=1)
    high_value = jnp.take(colormap_samples, index + 1, axis=1)
    return low_value + fraction[None] * (high_value - low_value)


def render(piece_samples, occupied_line_flags, slab_depth_rank, skew_offsets, colormap_samples, canvas_width, layers_overall):
    sheet_number, vertical_extent, horizontal_extent = piece_samples.shape

    def one_layer(carry, inputs):
        optical, colors = carry
        cells, layer_index = inputs
        values = transfer(cells, colormap_samples)
        absorb = values[3] * occupied_line_flags * (6.0 / layers_overall)
        opacity = 1.0 - jnp.exp(-absorb)
        offset = (((slab_depth_rank * sheet_number + layer_index) * skew_offsets) // layers_overall).astype(jnp.int32)
        stacked = jnp.concatenate([values[:3] * opacity[None], absorb[None]], axis=0)
        canvas = jnp.zeros((4, vertical_extent, canvas_width), piece_samples.dtype)
        canvas = lax.dynamic_update_slice(canvas, stacked, (jnp.int32(0), jnp.int32(0), offset))
        colors = colors + jnp.exp(-optical)[None] * canvas[:3]
        optical = optical + canvas[3]
        return (optical, colors), None

    start = (jnp.zeros((vertical_extent, canvas_width), piece_samples.dtype), jnp.zeros((3, vertical_extent, canvas_width), piece_samples.dtype))
    (optical, colors), unused = lax.scan(one_layer, start, (piece_samples, jnp.arange(sheet_number, dtype=jnp.int32)))
    return jnp.concatenate([colors, optical[None]], axis=0)


def composite(colors, depth_terms, sheetgroup_viewer_sequence):
    in_front = (sheetgroup_viewer_sequence[None, :] < sheetgroup_viewer_sequence[:, None]).astype(depth_terms.dtype)
    prefix = jnp.einsum('kj,jyx->kyx', in_front, depth_terms, precision=lax.Precision.HIGHEST)
    attenuate = jnp.exp(-prefix)
    shaded_color = jnp.sum(attenuate[None] * colors, axis=1)
    coverage = 1.0 - jnp.exp(-jnp.sum(depth_terms, axis=0))
    return jnp.concatenate([shaded_color, coverage[None]], axis=0)


def reference(thermal_grid, colormap_samples, sheetgroup_viewer_sequence, occupied_lines, skew_offsets):
    full_width = BX * N_REGION
    fragments = []
    for sheetgroup_place in range(N_DEPTH):
        piece_samples = thermal_grid[sheetgroup_place * PIECE_SHEETS:(sheetgroup_place + 1) * PIECE_SHEETS]
        interval_limits = jnp.repeat(occupied_lines[sheetgroup_place], BX)
        occupied_line_flags = (jnp.arange(PIECE_LINES, dtype=jnp.int32)[:, None] < interval_limits[None, :]).astype(thermal_grid.dtype)
        fragment_piece = render(piece_samples, occupied_line_flags, sheetgroup_viewer_sequence[sheetgroup_place], skew_offsets[0], colormap_samples, full_width + BX, SHEET_COUNT)
        fragments.append(fragment_piece[:, :, :full_width])
    stacked = jnp.stack(fragments, axis=1)
    return composite(stacked[:3], stacked[3], sheetgroup_viewer_sequence)
```

```python
import functools

import jax
import jax.numpy as jnp
from jax import lax
from jax.experimental import pallas as pl
from jax.experimental.pallas import tpu as pltpu
from jax.sharding import PartitionSpec as P

EMPTY = 1.0e6
LANES = 128
SUBLANES = 8


def lookup(cells, tables, knot_count):
    scaled = jnp.clip((cells + 3.0) * ((knot_count - 1) / 6.0), 0.0, knot_count - 1.0)
    lower = jnp.minimum(jnp.floor(scaled), knot_count - 2.0)
    fraction = scaled - lower
    index = lower.astype(jnp.int32)
    upper_half = index >= LANES
    lane = jnp.where(upper_half, index - LANES, index)
    values = []
    for c in range(4):
        picked = []
        for base in (0, 8):
            low = jnp.take_along_axis(tables[base + 2 * c], lane, axis=1, mode="promise_in_bounds")
            high = jnp.take_along_axis(tables[base + 2 * c + 1], lane, axis=1, mode="promise_in_bounds")
            picked.append(jnp.where(upper_half, high, low))
        values.append(picked[0] + fraction * picked[1])
    return values


def render_kernel(seq_ref, skew_ref, own_ref, left_ref, cmap_ref, out_ref, shifted_ref):
    layers, slabs, rows, width = own_ref.shape
    layers_overall = layers * slabs
    knot_count = cmap_ref.shape[1]
    first_tile = lax.axis_index("region") == 0
    skew = skew_ref[0]

    order = []
    for k in range(slabs):
        s = jnp.int32(0)
        for j in range(slabs):
            s = s + jnp.where(seq_ref[j] == k, j, 0)
        order.append(s)

    for k in range(slabs):
        s = order[k]
        for l in range(layers):
            shift = ((k * layers + l) * skew) // layers_overall
            for r in range(rows // SUBLANES):
                band = pl.ds(r * SUBLANES, SUBLANES)
                left = jnp.where(first_tile, EMPTY, left_ref[l, s, band, :])
                joined = jnp.concatenate([left, own_ref[l, s, band, :]], axis=1)
                shifted_ref[l, k, band, :] = pltpu.roll(joined, shift, 1)[:, width:]

    cmap = cmap_ref[...]
    following = pltpu.roll(cmap, knot_count - 1, 1)
    delta = following - cmap
    tables = []
    for src in (cmap, delta):
        for c in range(4):
            for h in range(knot_count // LANES):
                row = src[c : c + 1, h * LANES : (h + 1) * LANES]
                tables.append(jnp.broadcast_to(row, (SUBLANES, LANES)))

    pieces = width // LANES

    def block(i, carry):
        r = i // pieces
        j = i % pieces
        band = pl.ds(pl.multiple_of(r * SUBLANES, SUBLANES), SUBLANES)
        cols = pl.ds(pl.multiple_of(j * LANES, LANES), LANES)
        depth_sum = jnp.zeros((SUBLANES, LANES), jnp.float32)
        image = [jnp.zeros((SUBLANES, LANES), jnp.float32) for _ in range(3)]
        for k in range(slabs):
            tau = None
            color = None
            for l in range(layers):
                cells = shifted_ref[l, k, band, cols]
                values = lookup(cells, tables, knot_count)
                absorb = jnp.where(cells < 100.0, values[3] * (6.0 / layers_overall), 0.0)
                through = jnp.exp(-absorb)
                opacity = 1.0 - through
                emit = [values[c] * opacity for c in range(3)]
                if tau is None:
                    color = emit
                    tau = absorb
                else:
                    fade = jnp.exp(-tau)
                    color = [color[c] + fade * emit[c] for c in range(3)]
                    tau = tau + absorb
            if k == 0:
                image = color
            else:
                fade = jnp.exp(-depth_sum)
                image = [image[c] + fade * color[c] for c in range(3)]
            depth_sum = depth_sum + tau
        for c in range(3):
            out_ref[c, band, cols] = image[c]
        out_ref[3, band, cols] = 1.0 - jnp.exp(-depth_sum)
        return carry

    lax.fori_loop(0, (rows // SUBLANES) * pieces, block, 0)


def shards(thermal_grid, colormap_samples, sheetgroup_viewer_sequence, occupied_lines, skew_offsets):
    layers, rows, width = thermal_grid.shape
    slabs = lax.axis_size("depth")
    regions = lax.axis_size("region")
    share = rows // slabs
    line = lax.broadcasted_iota(jnp.int32, (1, rows, 1), 1)
    marked = jnp.where(line < occupied_lines[0, 0], thermal_grid, EMPTY)
    blocks = marked.reshape(layers, slabs, share, width)
    own = lax.all_to_all(blocks, "depth", split_axis=1, concat_axis=1, tiled=True)
    left = lax.ppermute(own, "region", [(i, i + 1) for i in range(regions - 1)])
    vmem = pltpu.VMEM
    smem = pltpu.SMEM
    return pl.pallas_call(
        render_kernel,
        out_shape=jax.ShapeDtypeStruct((4, share, width), jnp.float32),
        in_specs=[
            pl.BlockSpec(memory_space=smem),
            pl.BlockSpec(memory_space=smem),
            pl.BlockSpec(memory_space=vmem),
            pl.BlockSpec(memory_space=vmem),
            pl.BlockSpec(memory_space=vmem),
        ],
        out_specs=pl.BlockSpec(memory_space=vmem),
        scratch_shapes=[pltpu.VMEM((layers, slabs, share, width), jnp.float32)],
    )(sheetgroup_viewer_sequence, skew_offsets, own, left, colormap_samples)


def solution(mesh):
    in_specs = (P("depth", None, "region"), P(), P(), P("depth", "region"), P())
    out_specs = P(None, "depth", "region")
    return jax.shard_map(shards, mesh=mesh, in_specs=in_specs, out_specs=out_specs, check_vma=False)
```

```python
import functools

import jax
import jax.numpy as jnp
from jax import lax
from jax.experimental import pallas as pl
from jax.experimental.pallas import tpu as pltpu
from jax.sharding import PartitionSpec as P

EMPTY = 1.0e6
LANES = 128
SUBLANES = 8


def lookup(cells, tables, knot_count):
    scaled = jnp.clip((cells + 3.0) * ((knot_count - 1) / 6.0), 0.0, knot_count - 1.0)
    lower = jnp.minimum(jnp.floor(scaled), knot_count - 2.0)
    fraction = scaled - lower
    index = lower.astype(jnp.int32)
    upper_half = index >= LANES
    lane = jnp.where(upper_half, index - LANES, index)
    values = []
    for c in range(4):
        picked = []
        for base in (0, 8):
            low = jnp.take_along_axis(tables[base + 2 * c], lane, axis=1, mode="promise_in_bounds")
            high = jnp.take_along_axis(tables[base + 2 * c + 1], lane, axis=1, mode="promise_in_bounds")
            picked.append(jnp.where(upper_half, high, low))
        values.append(picked[0] + fraction * picked[1])
    return values


def render_kernel(seq_ref, skew_ref, own_ref, left_ref, cmap_ref, out_ref, shifted_ref):
    layers, slabs, rows, width = own_ref.shape
    layers_overall = layers * slabs
    knot_count = cmap_ref.shape[1]
    first_tile = lax.axis_index("region") == 0
    me = lax.axis_index("depth")
    skew = skew_ref[0]

    order = []
    for k in range(slabs):
        s = jnp.int32(0)
        for j in range(slabs):
            s = s + jnp.where(seq_ref[j] == k, j, 0)
        order.append((s - me + slabs) % slabs)

    for k in range(slabs):
        s = order[k]
        for l in range(layers):
            shift = ((k * layers + l) * skew) // layers_overall
            for r in range(rows // SUBLANES):
                band = pl.ds(r * SUBLANES, SUBLANES)
                left = jnp.where(first_tile, EMPTY, left_ref[l, s, band, :])
                joined = jnp.concatenate([left, own_ref[l, s, band, :]], axis=1)
                shifted_ref[l, k, band, :] = pltpu.roll(joined, shift, 1)[:, width:]

    cmap = cmap_ref[...]
    following = pltpu.roll(cmap, knot_count - 1, 1)
    delta = following - cmap
    tables = []
    for src in (cmap, delta):
        for c in range(4):
            for h in range(knot_count // LANES):
                row = src[c : c + 1, h * LANES : (h + 1) * LANES]
                tables.append(jnp.broadcast_to(row, (SUBLANES, LANES)))

    pieces = width // LANES

    def block(i, carry):
        r = i // pieces
        j = i % pieces
        band = pl.ds(pl.multiple_of(r * SUBLANES, SUBLANES), SUBLANES)
        cols = pl.ds(pl.multiple_of(j * LANES, LANES), LANES)
        depth_sum = jnp.zeros((SUBLANES, LANES), jnp.float32)
        image = [jnp.zeros((SUBLANES, LANES), jnp.float32) for _ in range(3)]
        for k in range(slabs):
            tau = None
            color = None
            for l in range(layers):
                cells = shifted_ref[l, k, band, cols]
                values = lookup(cells, tables, knot_count)
                absorb = jnp.where(cells < 100.0, values[3] * (6.0 / layers_overall), 0.0)
                through = jnp.exp(-absorb)
                opacity = 1.0 - through
                emit = [values[c] * opacity for c in range(3)]
                if tau is None:
                    color = emit
                    tau = absorb
                else:
                    fade = jnp.exp(-tau)
                    color = [color[c] + fade * emit[c] for c in range(3)]
                    tau = tau + absorb
            if k == 0:
                image = color
            else:
                fade = jnp.exp(-depth_sum)
                image = [image[c] + fade * color[c] for c in range(3)]
            depth_sum = depth_sum + tau
        for c in range(3):
            out_ref[c, band, cols] = image[c]
        out_ref[3, band, cols] = 1.0 - jnp.exp(-depth_sum)
        return carry

    lax.fori_loop(0, (rows // SUBLANES) * pieces, block, 0)


def shards(thermal_grid, colormap_samples, sheetgroup_viewer_sequence, occupied_lines, skew_offsets):
    layers, rows, width = thermal_grid.shape
    slabs = lax.axis_size("depth")
    regions = lax.axis_size("region")
    share = rows // slabs
    line = lax.broadcasted_iota(jnp.int32, (1, rows, 1), 1)
    marked = jnp.where(line < occupied_lines[0, 0], thermal_grid, EMPTY)
    blocks = marked.reshape(layers, slabs, share, width)
    me = lax.axis_index("depth")
    held = [blocks[:, me]]
    for m in range(1, slabs):
        piece = lax.dynamic_index_in_dim(blocks, (me - m) % slabs, axis=1, keepdims=False)
        route = [(i, (i - m) % slabs) for i in range(slabs)]
        held.append(lax.ppermute(piece, "depth", route))
    own = jnp.stack(held, axis=1)
    left = lax.ppermute(own, "region", [(i, i + 1) for i in range(regions - 1)])
    vmem = pltpu.VMEM
    smem = pltpu.SMEM
    return pl.pallas_call(
        render_kernel,
        out_shape=jax.ShapeDtypeStruct((4, share, width), jnp.float32),
        in_specs=[
            pl.BlockSpec(memory_space=smem),
            pl.BlockSpec(memory_space=smem),
            pl.BlockSpec(memory_space=vmem),
            pl.BlockSpec(memory_space=vmem),
            pl.BlockSpec(memory_space=vmem),
        ],
        out_specs=pl.BlockSpec(memory_space=vmem),
        scratch_shapes=[pltpu.VMEM((layers, slabs, share, width), jnp.float32)],
    )(sheetgroup_viewer_sequence, skew_offsets, own, left, colormap_samples)


def solution(mesh):
    in_specs = (P("depth", None, "region"), P(), P(), P("depth", "region"), P())
    out_specs = P(None, "depth", "region")
    return jax.shard_map(shards, mesh=mesh, in_specs=in_specs, out_specs=out_specs, check_vma=False)
```

```python
import functools

import jax
import jax.numpy as jnp
from jax import lax
from jax.experimental import pallas as pl
from jax.experimental.pallas import tpu as pltpu
from jax.sharding import PartitionSpec as P

EMPTY = 1.0e6
LANES = 128
SUBLANES = 8


def lookup(cells, tables, knot_count):
    scaled = jnp.clip((cells + 3.0) * ((knot_count - 1) / 6.0), 0.0, knot_count - 1.0)
    lower = jnp.minimum(jnp.floor(scaled), knot_count - 2.0)
    fraction = scaled - lower
    index = lower.astype(jnp.int32)
    upper_half = index >= LANES
    lane = jnp.where(upper_half, index - LANES, index)
    values = []
    for c in range(4):
        picked = []
        for base in (0, 8):
            low = jnp.take_along_axis(tables[base + 2 * c], lane, axis=1, mode="promise_in_bounds")
            high = jnp.take_along_axis(tables[base + 2 * c + 1], lane, axis=1, mode="promise_in_bounds")
            picked.append(jnp.where(upper_half, high, low))
        values.append(picked[0] + fraction * picked[1])
    return values


def slab_kernel(slot, seq_ref, skew_ref, own_ref, left_ref, cmap_ref, out_ref, shifted_ref):
    layers, rows, width = own_ref.shape
    slabs = seq_ref.shape[0]
    layers_overall = layers * slabs
    knot_count = cmap_ref.shape[1]
    first_tile = lax.axis_index("region") == 0
    rank = seq_ref[(lax.axis_index("depth") + slot) % slabs]
    skew = skew_ref[0]

    for l in range(layers):
        shift = ((rank * layers + l) * skew) // layers_overall
        for r in range(rows // SUBLANES):
            band = pl.ds(r * SUBLANES, SUBLANES)
            left = jnp.where(first_tile, EMPTY, left_ref[l, band, :])
            joined = jnp.concatenate([left, own_ref[l, band, :]], axis=1)
            shifted_ref[l, band, :] = pltpu.roll(joined, shift, 1)[:, width:]

    cmap = cmap_ref[...]
    following = pltpu.roll(cmap, knot_count - 1, 1)
    delta = following - cmap
    tables = []
    for src in (cmap, delta):
        for c in range(4):
            for h in range(knot_count // LANES):
                row = src[c : c + 1, h * LANES : (h + 1) * LANES]
                tables.append(jnp.broadcast_to(row, (SUBLANES, LANES)))

    pieces = width // LANES

    def block(i, carry):
        band = pl.ds(pl.multiple_of((i // pieces) * SUBLANES, SUBLANES), SUBLANES)
        cols = pl.ds(pl.multiple_of((i % pieces) * LANES, LANES), LANES)
        tau = None
        color = None
        for l in range(layers):
            cells = shifted_ref[l, band, cols]
            values = lookup(cells, tables, knot_count)
            absorb = jnp.where(cells < 100.0, values[3] * (6.0 / layers_overall), 0.0)
            opacity = 1.0 - jnp.exp(-absorb)
            emit = [values[c] * opacity for c in range(3)]
            if tau is None:
                color = emit
                tau = absorb
            else:
                fade = jnp.exp(-tau)
                color = [color[c] + fade * emit[c] for c in range(3)]
                tau = tau + absorb
        for c in range(3):
            out_ref[c, band, cols] = color[c]
        out_ref[3, band, cols] = tau
        return carry

    lax.fori_loop(0, (rows // SUBLANES) * pieces, block, 0)


def composite_kernel(seq_ref, *refs):
    parts, out_ref = refs[:-1], refs[-1]
    slabs = len(parts)
    me = lax.axis_index("depth")
    ranks = [seq_ref[(me + m) % slabs] for m in range(slabs)]
    _, rows, width = out_ref.shape
    pieces = width // LANES

    def block(i, carry):
        band = pl.ds(pl.multiple_of((i // pieces) * SUBLANES, SUBLANES), SUBLANES)
        cols = pl.ds(pl.multiple_of((i % pieces) * LANES, LANES), LANES)
        taus = [part[3, band, cols] for part in parts]
        image = [None] * 3
        total = None
        for m in range(slabs):
            prefix = None
            for j in range(slabs):
                if j == m:
                    continue
                term = jnp.where(ranks[j] < ranks[m], 1.0, 0.0) * taus[j]
                prefix = term if prefix is None else prefix + term
            fade = jnp.exp(-prefix) if prefix is not None else 1.0
            for c in range(3):
                shaded = fade * parts[m][c, band, cols]
                image[c] = shaded if image[c] is None else image[c] + shaded
            total = taus[m] if total is None else total + taus[m]
        for c in range(3):
            out_ref[c, band, cols] = image[c]
        out_ref[3, band, cols] = 1.0 - jnp.exp(-total)
        return carry

    lax.fori_loop(0, (rows // SUBLANES) * pieces, block, 0)


def shards(thermal_grid, colormap_samples, sheetgroup_viewer_sequence, occupied_lines, skew_offsets):
    layers, rows, width = thermal_grid.shape
    slabs = lax.axis_size("depth")
    regions = lax.axis_size("region")
    share = rows // slabs
    line = lax.broadcasted_iota(jnp.int32, (1, rows, 1), 1)
    marked = jnp.where(line < occupied_lines[0, 0], thermal_grid, EMPTY)
    blocks = marked.reshape(layers, slabs, share, width)
    me = lax.axis_index("depth")
    to_right = [(i, i + 1) for i in range(regions - 1)]
    smem = pl.BlockSpec(memory_space=pltpu.SMEM)
    vmem = pl.BlockSpec(memory_space=pltpu.VMEM)
    slab_parts = []
    for m in range(slabs):
        piece = lax.dynamic_index_in_dim(blocks, (me - m) % slabs, axis=1, keepdims=False)
        if m > 0:
            piece = lax.ppermute(piece, "depth", [(i, (i - m) % slabs) for i in range(slabs)])
        left = lax.ppermute(piece, "region", to_right)
        slab_parts.append(
            pl.pallas_call(
                functools.partial(slab_kernel, m),
                out_shape=jax.ShapeDtypeStruct((4, share, width), jnp.float32),
                in_specs=[smem, smem, vmem, vmem, vmem],
                out_specs=vmem,
                scratch_shapes=[pltpu.VMEM((layers, share, width), jnp.float32)],
            )(sheetgroup_viewer_sequence, skew_offsets, piece, left, colormap_samples)
        )
    return pl.pallas_call(
        composite_kernel,
        out_shape=jax.ShapeDtypeStruct((4, share, width), jnp.float32),
        in_specs=[smem] + [vmem] * slabs,
        out_specs=vmem,
    )(sheetgroup_viewer_sequence, *slab_parts)


def solution(mesh):
    in_specs = (P("depth", None, "region"), P(), P(), P("depth", "region"), P())
    out_specs = P(None, "depth", "region")
    return jax.shard_map(shards, mesh=mesh, in_specs=in_specs, out_specs=out_specs, check_vma=False)
```

```python
import functools

import jax
import jax.numpy as jnp
from jax import lax
from jax.experimental import pallas as pl
from jax.experimental.pallas import tpu as pltpu
from jax.sharding import PartitionSpec as P

EMPTY = 1.0e6
LANES = 128
SUBLANES = 8


def lookup(cells, tables, knot_count):
    scaled = jnp.clip((cells + 3.0) * ((knot_count - 1) / 6.0), 0.0, knot_count - 1.0)
    lower = jnp.minimum(jnp.floor(scaled), knot_count - 2.0)
    fraction = scaled - lower
    index = lower.astype(jnp.int32)
    upper_half = index >= LANES
    lane = jnp.where(upper_half, index - LANES, index)
    values = []
    for c in range(4):
        picked = []
        for base in (0, 8):
            low = jnp.take_along_axis(tables[base + 2 * c], lane, axis=1, mode="promise_in_bounds")
            high = jnp.take_along_axis(tables[base + 2 * c + 1], lane, axis=1, mode="promise_in_bounds")
            picked.append(jnp.where(upper_half, high, low))
        values.append(picked[0] + fraction * picked[1])
    return values


def render_kernel(seq_ref, skew_ref, own_ref, left_ref, cmap_ref, out_ref, shifted_ref):
    layers, slabs, rows, width = own_ref.shape
    layers_overall = layers * slabs
    knot_count = cmap_ref.shape[1]
    first_tile = lax.axis_index("region") == 0
    me = lax.axis_index("depth")
    skew = skew_ref[0]

    order = []
    for k in range(slabs):
        s = jnp.int32(0)
        for j in range(slabs):
            s = s + jnp.where(seq_ref[j] == k, j, 0)
        order.append((s - me + slabs) % slabs)

    for k in range(slabs):
        s = order[k]
        for l in range(layers):
            shift = ((k * layers + l) * skew) // layers_overall
            for r in range(rows // SUBLANES):
                band = pl.ds(r * SUBLANES, SUBLANES)
                left = jnp.where(first_tile, EMPTY, left_ref[l, s, band, :])
                joined = jnp.concatenate([left, own_ref[l, s, band, :]], axis=1)
                shifted_ref[l, k, band, :] = pltpu.roll(joined, shift, 1)[:, width:]

    cmap = cmap_ref[...]
    following = pltpu.roll(cmap, knot_count - 1, 1)
    delta = following - cmap
    tables = []
    for src in (cmap, delta):
        for c in range(4):
            for h in range(knot_count // LANES):
                row = src[c : c + 1, h * LANES : (h + 1) * LANES]
                tables.append(jnp.broadcast_to(row, (SUBLANES, LANES)))

    pieces = width // LANES

    def block(i, carry):
        r = i // pieces
        j = i % pieces
        band = pl.ds(pl.multiple_of(r * SUBLANES, SUBLANES), SUBLANES)
        cols = pl.ds(pl.multiple_of(j * LANES, LANES), LANES)
        depth_sum = jnp.zeros((SUBLANES, LANES), jnp.float32)
        image = [jnp.zeros((SUBLANES, LANES), jnp.float32) for _ in range(3)]
        for k in range(slabs):
            tau = None
            color = None
            for l in range(layers):
                cells = shifted_ref[l, k, band, cols]
                values = lookup(cells, tables, knot_count)
                absorb = jnp.where(cells < 100.0, values[3] * (6.0 / layers_overall), 0.0)
                through = jnp.exp(-absorb)
                opacity = 1.0 - through
                emit = [values[c] * opacity for c in range(3)]
                if tau is None:
                    color = emit
                    tau = absorb
                else:
                    fade = jnp.exp(-tau)
                    color = [color[c] + fade * emit[c] for c in range(3)]
                    tau = tau + absorb
            if k == 0:
                image = color
            else:
                fade = jnp.exp(-depth_sum)
                image = [image[c] + fade * color[c] for c in range(3)]
            depth_sum = depth_sum + tau
        for c in range(3):
            out_ref[c, band, cols] = image[c]
        out_ref[3, band, cols] = 1.0 - jnp.exp(-depth_sum)
        return carry

    lax.fori_loop(0, (rows // SUBLANES) * pieces, block, 0)


def shards(thermal_grid, colormap_samples, sheetgroup_viewer_sequence, occupied_lines, skew_offsets):
    layers, rows, width = thermal_grid.shape
    slabs = lax.axis_size("depth")
    regions = lax.axis_size("region")
    share = rows // slabs
    me = lax.axis_index("depth")
    line = lax.broadcasted_iota(jnp.int32, (1, share, 1), 1)
    held = []
    for m in range(slabs):
        start = ((me - m) % slabs) * share
        piece = lax.dynamic_slice_in_dim(thermal_grid, start, share, axis=1)
        piece = jnp.where(start + line < occupied_lines[0, 0], piece, EMPTY)
        if m > 0:
            piece = lax.ppermute(piece, "depth", [(i, (i - m) % slabs) for i in range(slabs)])
        held.append(piece)
    own = jnp.stack(held, axis=1)
    left = lax.ppermute(own, "region", [(i, i + 1) for i in range(regions - 1)])
    vmem = pltpu.VMEM
    smem = pltpu.SMEM
    return pl.pallas_call(
        render_kernel,
        out_shape=jax.ShapeDtypeStruct((4, share, width), jnp.float32),
        in_specs=[
            pl.BlockSpec(memory_space=smem),
            pl.BlockSpec(memory_space=smem),
            pl.BlockSpec(memory_space=vmem),
            pl.BlockSpec(memory_space=vmem),
            pl.BlockSpec(memory_space=vmem),
        ],
        out_specs=pl.BlockSpec(memory_space=vmem),
        scratch_shapes=[pltpu.VMEM((layers, slabs, share, width), jnp.float32)],
    )(sheetgroup_viewer_sequence, skew_offsets, own, left, colormap_samples)


def solution(mesh):
    in_specs = (P("depth", None, "region"), P(), P(), P("depth", "region"), P())
    out_specs = P(None, "depth", "region")
    return jax.shard_map(shards, mesh=mesh, in_specs=in_specs, out_specs=out_specs, check_vma=False)
```

```python
import functools

import jax
import jax.numpy as jnp
from jax import lax
from jax.experimental import pallas as pl
from jax.experimental.pallas import tpu as pltpu
from jax.sharding import PartitionSpec as P

EMPTY = 1.0e6
LANES = 128
SUBLANES = 8


def lookup(cells, tables, knot_count):
    scaled = jnp.clip((cells + 3.0) * ((knot_count - 1) / 6.0), 0.0, knot_count - 1.0)
    lower = jnp.minimum(jnp.floor(scaled), knot_count - 2.0)
    fraction = scaled - lower
    index = lower.astype(jnp.int32)
    upper_half = index >= LANES
    lane = jnp.where(upper_half, index - LANES, index)
    values = []
    for c in range(4):
        picked = []
        for base in (0, 8):
            low = jnp.take_along_axis(tables[base + 2 * c], lane, axis=1, mode="promise_in_bounds")
            high = jnp.take_along_axis(tables[base + 2 * c + 1], lane, axis=1, mode="promise_in_bounds")
            picked.append(jnp.where(upper_half, high, low))
        values.append(picked[0] + fraction * picked[1])
    return values


def render_kernel(seq_ref, skew_ref, *refs):
    halves = (len(refs) - 3) // 2
    own_refs, left_refs = refs[:halves], refs[halves : 2 * halves]
    cmap_ref, out_ref, shifted_ref = refs[2 * halves :]
    layers, slabs, half_rows, width = own_refs[0].shape
    rows = half_rows * halves
    layers_overall = layers * slabs
    knot_count = cmap_ref.shape[1]
    first_tile = lax.axis_index("region") == 0
    me = lax.axis_index("depth")
    skew = skew_ref[0]

    order = []
    for k in range(slabs):
        s = jnp.int32(0)
        for j in range(slabs):
            s = s + jnp.where(seq_ref[j] == k, j, 0)
        order.append((s - me + slabs) % slabs)

    for k in range(slabs):
        s = order[k]
        for l in range(layers):
            shift = ((k * layers + l) * skew) // layers_overall
            for r in range(rows // SUBLANES):
                band = pl.ds(r * SUBLANES, SUBLANES)
                c, rest = divmod(r * SUBLANES, half_rows)
                part = pl.ds(rest, SUBLANES)
                left = jnp.where(first_tile, EMPTY, left_refs[c][l, s, part, :])
                joined = jnp.concatenate([left, own_refs[c][l, s, part, :]], axis=1)
                shifted_ref[l, k, band, :] = pltpu.roll(joined, shift, 1)[:, width:]

    cmap = cmap_ref[...]
    following = pltpu.roll(cmap, knot_count - 1, 1)
    delta = following - cmap
    tables = []
    for src in (cmap, delta):
        for c in range(4):
            for h in range(knot_count // LANES):
                row = src[c : c + 1, h * LANES : (h + 1) * LANES]
                tables.append(jnp.broadcast_to(row, (SUBLANES, LANES)))

    pieces = width // LANES

    def block(i, carry):
        r = i // pieces
        j = i % pieces
        band = pl.ds(pl.multiple_of(r * SUBLANES, SUBLANES), SUBLANES)
        cols = pl.ds(pl.multiple_of(j * LANES, LANES), LANES)
        depth_sum = jnp.zeros((SUBLANES, LANES), jnp.float32)
        image = [jnp.zeros((SUBLANES, LANES), jnp.float32) for _ in range(3)]
        for k in range(slabs):
            tau = None
            color = None
            for l in range(layers):
                cells = shifted_ref[l, k, band, cols]
                values = lookup(cells, tables, knot_count)
                absorb = jnp.where(cells < 100.0, values[3] * (6.0 / layers_overall), 0.0)
                through = jnp.exp(-absorb)
                opacity = 1.0 - through
                emit = [values[c] * opacity for c in range(3)]
                if tau is None:
                    color = emit
                    tau = absorb
                else:
                    fade = jnp.exp(-tau)
                    color = [color[c] + fade * emit[c] for c in range(3)]
                    tau = tau + absorb
            if k == 0:
                image = color
            else:
                fade = jnp.exp(-depth_sum)
                image = [image[c] + fade * color[c] for c in range(3)]
            depth_sum = depth_sum + tau
        for c in range(3):
            out_ref[c, band, cols] = image[c]
        out_ref[3, band, cols] = 1.0 - jnp.exp(-depth_sum)
        return carry

    lax.fori_loop(0, (rows // SUBLANES) * pieces, block, 0)


def shards(thermal_grid, colormap_samples, sheetgroup_viewer_sequence, occupied_lines, skew_offsets):
    layers, rows, width = thermal_grid.shape
    slabs = lax.axis_size("depth")
    regions = lax.axis_size("region")
    share = rows // slabs
    me = lax.axis_index("depth")
    halves = 2 if share % (2 * SUBLANES) == 0 else 1
    half = share // halves
    line = lax.broadcasted_iota(jnp.int32, (1, half, 1), 1)
    owns, lefts = [], []
    for c in range(halves):
        held = []
        for m in range(slabs):
            start = ((me - m) % slabs) * share + c * half
            piece = lax.dynamic_slice_in_dim(thermal_grid, start, half, axis=1)
            piece = jnp.where(start + line < occupied_lines[0, 0], piece, EMPTY)
            if m > 0:
                piece = lax.ppermute(piece, "depth", [(i, (i - m) % slabs) for i in range(slabs)])
            held.append(piece)
        own = jnp.stack(held, axis=1)
        owns.append(own)
        lefts.append(lax.ppermute(own, "region", [(i, i + 1) for i in range(regions - 1)]))
    vmem = pltpu.VMEM
    smem = pltpu.SMEM
    return pl.pallas_call(
        render_kernel,
        out_shape=jax.ShapeDtypeStruct((4, share, width), jnp.float32),
        in_specs=[
            pl.BlockSpec(memory_space=smem),
            pl.BlockSpec(memory_space=smem),
        ]
        + [pl.BlockSpec(memory_space=vmem)] * (2 * halves + 1),
        out_specs=pl.BlockSpec(memory_space=vmem),
        scratch_shapes=[pltpu.VMEM((layers, slabs, share, width), jnp.float32)],
    )(sheetgroup_viewer_sequence, skew_offsets, *owns, *lefts, colormap_samples)


def solution(mesh):
    in_specs = (P("depth", None, "region"), P(), P(), P("depth", "region"), P())
    out_specs = P(None, "depth", "region")
    return jax.shard_map(shards, mesh=mesh, in_specs=in_specs, out_specs=out_specs, check_vma=False)
```

```python
import functools

import jax
import jax.numpy as jnp
from jax import lax
from jax.experimental import pallas as pl
from jax.experimental.pallas import tpu as pltpu
from jax.sharding import PartitionSpec as P

EMPTY = 1.0e6
LANES = 128
SUBLANES = 8


def lookup(cells, tables, knot_count):
    scaled = jnp.clip((cells + 3.0) * ((knot_count - 1) / 6.0), 0.0, knot_count - 1.0)
    lower = jnp.minimum(jnp.floor(scaled), knot_count - 2.0)
    fraction = scaled - lower
    index = lower.astype(jnp.int32)
    upper_half = index >= LANES
    lane = jnp.where(upper_half, index - LANES, index)
    values = []
    for c in range(4):
        picked = []
        for base in (0, 8):
            low = jnp.take_along_axis(tables[base + 2 * c], lane, axis=1, mode="promise_in_bounds")
            high = jnp.take_along_axis(tables[base + 2 * c + 1], lane, axis=1, mode="promise_in_bounds")
            picked.append(jnp.where(upper_half, high, low))
        values.append(picked[0] + fraction * picked[1])
    return values


def render_kernel(seq_ref, skew_ref, *refs):
    halves = (len(refs) - 3) // 2
    own_refs, left_refs = refs[:halves], refs[halves : 2 * halves]
    cmap_ref, out_ref, shifted_ref = refs[2 * halves :]
    slabs, layers, half_rows, width = own_refs[0].shape
    rows = half_rows * halves
    layers_overall = layers * slabs
    knot_count = cmap_ref.shape[1]
    first_tile = lax.axis_index("region") == 0
    me = lax.axis_index("depth")
    skew = skew_ref[0]

    order = []
    for k in range(slabs):
        s = jnp.int32(0)
        for j in range(slabs):
            s = s + jnp.where(seq_ref[j] == k, j, 0)
        order.append((s - me + slabs) % slabs)

    for k in range(slabs):
        s = order[k]
        for l in range(layers):
            shift = ((k * layers + l) * skew) // layers_overall
            for r in range(rows // SUBLANES):
                band = pl.ds(r * SUBLANES, SUBLANES)
                c, rest = divmod(r * SUBLANES, half_rows)
                part = pl.ds(rest, SUBLANES)
                left = jnp.where(first_tile, EMPTY, left_refs[c][s, l, part, :])
                joined = jnp.concatenate([left, own_refs[c][s, l, part, :]], axis=1)
                shifted_ref[l, k, band, :] = pltpu.roll(joined, shift, 1)[:, width:]

    cmap = cmap_ref[...]
    following = pltpu.roll(cmap, knot_count - 1, 1)
    delta = following - cmap
    tables = []
    for src in (cmap, delta):
        for c in range(4):
            for h in range(knot_count // LANES):
                row = src[c : c + 1, h * LANES : (h + 1) * LANES]
                tables.append(jnp.broadcast_to(row, (SUBLANES, LANES)))

    pieces = width // LANES

    def block(i, carry):
        r = i // pieces
        j = i % pieces
        band = pl.ds(pl.multiple_of(r * SUBLANES, SUBLANES), SUBLANES)
        cols = pl.ds(pl.multiple_of(j * LANES, LANES), LANES)
        depth_sum = jnp.zeros((SUBLANES, LANES), jnp.float32)
        image = [jnp.zeros((SUBLANES, LANES), jnp.float32) for _ in range(3)]
        for k in range(slabs):
            tau = None
            color = None
            for l in range(layers):
                cells = shifted_ref[l, k, band, cols]
                values = lookup(cells, tables, knot_count)
                absorb = jnp.where(cells < 100.0, values[3] * (6.0 / layers_overall), 0.0)
                through = jnp.exp(-absorb)
                opacity = 1.0 - through
                emit = [values[c] * opacity for c in range(3)]
                if tau is None:
                    color = emit
                    tau = absorb
                else:
                    fade = jnp.exp(-tau)
                    color = [color[c] + fade * emit[c] for c in range(3)]
                    tau = tau + absorb
            if k == 0:
                image = color
            else:
                fade = jnp.exp(-depth_sum)
                image = [image[c] + fade * color[c] for c in range(3)]
            depth_sum = depth_sum + tau
        for c in range(3):
            out_ref[c, band, cols] = image[c]
        out_ref[3, band, cols] = 1.0 - jnp.exp(-depth_sum)
        return carry

    lax.fori_loop(0, (rows // SUBLANES) * pieces, block, 0)


def shards(thermal_grid, colormap_samples, sheetgroup_viewer_sequence, occupied_lines, skew_offsets):
    layers, rows, width = thermal_grid.shape
    slabs = lax.axis_size("depth")
    regions = lax.axis_size("region")
    share = rows // slabs
    me = lax.axis_index("depth")
    halves = 2 if share % (2 * SUBLANES) == 0 else 1
    half = share // halves
    line = lax.broadcasted_iota(jnp.int32, (1, half, 1), 1)
    owns, lefts = [], []
    for c in range(halves):
        held = []
        for m in range(slabs):
            start = ((me - m) % slabs) * share + c * half
            piece = lax.dynamic_slice_in_dim(thermal_grid, start, half, axis=1)
            piece = jnp.where(start + line < occupied_lines[0, 0], piece, EMPTY)
            if m > 0:
                piece = lax.ppermute(piece, "depth", [(i, (i - m) % slabs) for i in range(slabs)])
            held.append(piece)
        own = jnp.stack(held, axis=0)
        owns.append(own)
        lefts.append(lax.ppermute(own, "region", [(i, i + 1) for i in range(regions - 1)]))
    vmem = pltpu.VMEM
    smem = pltpu.SMEM
    placed = [pltpu.with_memory_space_constraint(x, vmem) for x in owns + lefts]
    return pl.pallas_call(
        render_kernel,
        out_shape=jax.ShapeDtypeStruct((4, share, width), jnp.float32),
        in_specs=[
            pl.BlockSpec(memory_space=smem),
            pl.BlockSpec(memory_space=smem),
        ]
        + [pl.BlockSpec(memory_space=vmem)] * (2 * halves + 1),
        out_specs=pl.BlockSpec(memory_space=vmem),
        scratch_shapes=[pltpu.VMEM((layers, slabs, share, width), jnp.float32)],
    )(sheetgroup_viewer_sequence, skew_offsets, *placed, colormap_samples)


def solution(mesh):
    in_specs = (P("depth", None, "region"), P(), P(), P("depth", "region"), P())
    out_specs = P(None, "depth", "region")
    return jax.shard_map(shards, mesh=mesh, in_specs=in_specs, out_specs=out_specs, check_vma=False)
```

```python
import functools

import jax
import jax.numpy as jnp
from jax import lax
from jax.experimental import pallas as pl
from jax.experimental.pallas import tpu as pltpu
from jax.sharding import PartitionSpec as P

EMPTY = 1.0e6
LANES = 128
SUBLANES = 8


def lookup(cells, tables, knot_count):
    scaled = jnp.clip((cells + 3.0) * ((knot_count - 1) / 6.0), 0.0, knot_count - 1.0)
    lower = jnp.minimum(jnp.floor(scaled), knot_count - 2.0)
    fraction = scaled - lower
    index = lower.astype(jnp.int32)
    upper_half = index >= LANES
    lane = jnp.where(upper_half, index - LANES, index)
    values = []
    for c in range(4):
        picked = []
        for base in (0, 8):
            low = jnp.take_along_axis(tables[base + 2 * c], lane, axis=1, mode="promise_in_bounds")
            high = jnp.take_along_axis(tables[base + 2 * c + 1], lane, axis=1, mode="promise_in_bounds")
            picked.append(jnp.where(upper_half, high, low))
        values.append(picked[0] + fraction * picked[1])
    return values


def render_kernel(seq_ref, skew_ref, *refs):
    halves = (len(refs) - 3) // 2
    own_refs, left_refs = refs[:halves], refs[halves : 2 * halves]
    cmap_ref, out_ref, shifted_ref = refs[2 * halves :]
    slabs, layers, half_rows, width = own_refs[0].shape
    rows = half_rows * halves
    layers_overall = layers * slabs
    knot_count = cmap_ref.shape[1]
    first_tile = lax.axis_index("region") == 0
    me = lax.axis_index("depth")
    skew = skew_ref[0]

    order = []
    for k in range(slabs):
        s = jnp.int32(0)
        for j in range(slabs):
            s = s + jnp.where(seq_ref[j] == k, j, 0)
        order.append((s - me + slabs) % slabs)

    for k in range(slabs):
        s = order[k]
        for l in range(layers):
            shift = ((k * layers + l) * skew) // layers_overall
            for r in range(rows // SUBLANES):
                band = pl.ds(r * SUBLANES, SUBLANES)
                c, rest = divmod(r * SUBLANES, half_rows)
                part = pl.ds(rest, SUBLANES)
                left = jnp.where(first_tile, EMPTY, left_refs[c][s, l, part, :])
                joined = jnp.concatenate([left, own_refs[c][s, l, part, :]], axis=1)
                shifted_ref[l, k, band, :] = pltpu.roll(joined, shift, 1)[:, width:]

    cmap = cmap_ref[...]
    following = pltpu.roll(cmap, knot_count - 1, 1)
    delta = following - cmap
    tables = []
    for src in (cmap, delta):
        for c in range(4):
            for h in range(knot_count // LANES):
                row = src[c : c + 1, h * LANES : (h + 1) * LANES]
                tables.append(jnp.broadcast_to(row, (SUBLANES, LANES)))

    pieces = width // LANES

    def block(i, carry):
        r = i // pieces
        j = i % pieces
        band = pl.ds(pl.multiple_of(r * SUBLANES, SUBLANES), SUBLANES)
        cols = pl.ds(pl.multiple_of(j * LANES, LANES), LANES)
        depth_sum = jnp.zeros((SUBLANES, LANES), jnp.float32)
        image = [jnp.zeros((SUBLANES, LANES), jnp.float32) for _ in range(3)]
        for k in range(slabs):
            tau = None
            color = None
            for l in range(layers):
                cells = shifted_ref[l, k, band, cols]
                values = lookup(cells, tables, knot_count)
                absorb = jnp.where(cells < 100.0, values[3] * (6.0 / layers_overall), 0.0)
                through = jnp.exp(-absorb)
                opacity = 1.0 - through
                emit = [values[c] * opacity for c in range(3)]
                if tau is None:
                    color = emit
                    tau = absorb
                else:
                    fade = jnp.exp(-tau)
                    color = [color[c] + fade * emit[c] for c in range(3)]
                    tau = tau + absorb
            if k == 0:
                image = color
            else:
                fade = jnp.exp(-depth_sum)
                image = [image[c] + fade * color[c] for c in range(3)]
            depth_sum = depth_sum + tau
        for c in range(3):
            out_ref[c, band, cols] = image[c]
        out_ref[3, band, cols] = 1.0 - jnp.exp(-depth_sum)
        return carry

    lax.fori_loop(0, (rows // SUBLANES) * pieces, block, 0)


def shards(thermal_grid, colormap_samples, sheetgroup_viewer_sequence, occupied_lines, skew_offsets):
    layers, rows, width = thermal_grid.shape
    slabs = lax.axis_size("depth")
    regions = lax.axis_size("region")
    share = rows // slabs
    me = lax.axis_index("depth")
    halves = max(1, min(4, share // SUBLANES))
    half = share // halves
    line = lax.broadcasted_iota(jnp.int32, (1, half, 1), 1)
    owns, lefts = [], []
    for c in range(halves):
        held = []
        for m in range(slabs):
            start = ((me - m) % slabs) * share + c * half
            piece = lax.dynamic_slice_in_dim(thermal_grid, start, half, axis=1)
            piece = jnp.where(start + line < occupied_lines[0, 0], piece, EMPTY)
            if m > 0:
                piece = lax.ppermute(piece, "depth", [(i, (i - m) % slabs) for i in range(slabs)])
            held.append(piece)
        own = jnp.stack(held, axis=0)
        owns.append(own)
        lefts.append(lax.ppermute(own, "region", [(i, i + 1) for i in range(regions - 1)]))
    vmem = pltpu.VMEM
    smem = pltpu.SMEM
    placed = [pltpu.with_memory_space_constraint(x, vmem) for x in owns + lefts]
    return pl.pallas_call(
        render_kernel,
        out_shape=jax.ShapeDtypeStruct((4, share, width), jnp.float32),
        in_specs=[
            pl.BlockSpec(memory_space=smem),
            pl.BlockSpec(memory_space=smem),
        ]
        + [pl.BlockSpec(memory_space=vmem)] * (2 * halves + 1),
        out_specs=pl.BlockSpec(memory_space=vmem),
        scratch_shapes=[pltpu.VMEM((layers, slabs, share, width), jnp.float32)],
    )(sheetgroup_viewer_sequence, skew_offsets, *placed, colormap_samples)


def solution(mesh):
    in_specs = (P("depth", None, "region"), P(), P(), P("depth", "region"), P())
    out_specs = P(None, "depth", "region")
    return jax.shard_map(shards, mesh=mesh, in_specs=in_specs, out_specs=out_specs, check_vma=False)
```

```python
import functools

import jax
import jax.numpy as jnp
from jax import lax
from jax.experimental import pallas as pl
from jax.experimental.pallas import tpu as pltpu
from jax.sharding import PartitionSpec as P

EMPTY = 1.0e6
LANES = 128
SUBLANES = 8


def lookup(cells, tables, knot_count):
    scaled = jnp.clip((cells + 3.0) * ((knot_count - 1) / 6.0), 0.0, knot_count - 1.0)
    lower = jnp.minimum(jnp.floor(scaled), knot_count - 2.0)
    fraction = scaled - lower
    index = lower.astype(jnp.int32)
    upper_half = index >= LANES
    lane = jnp.where(upper_half, index - LANES, index)
    values = []
    for c in range(4):
        picked = []
        for base in (0, 8):
            low = jnp.take_along_axis(tables[base + 2 * c], lane, axis=1, mode="promise_in_bounds")
            high = jnp.take_along_axis(tables[base + 2 * c + 1], lane, axis=1, mode="promise_in_bounds")
            picked.append(jnp.where(upper_half, high, low))
        values.append(picked[0] + fraction * picked[1])
    return values


def render_kernel(seq_ref, skew_ref, *refs):
    halves = (len(refs) - 3) // 2
    own_refs, left_refs = refs[:halves], refs[halves : 2 * halves]
    cmap_ref, out_ref, shifted_ref = refs[2 * halves :]
    slabs, layers, half_rows, width = own_refs[0].shape
    rows = half_rows * halves
    layers_overall = layers * slabs
    knot_count = cmap_ref.shape[1]
    first_tile = lax.axis_index("region") == 0
    me = lax.axis_index("depth")
    skew = skew_ref[0]

    order = []
    for k in range(slabs):
        s = jnp.int32(0)
        for j in range(slabs):
            s = s + jnp.where(seq_ref[j] == k, j, 0)
        order.append((s - me + slabs) % slabs)

    for k in range(slabs):
        s = order[k]
        for l in range(layers):
            shift = ((k * layers + l) * skew) // layers_overall
            for r in range(rows // SUBLANES):
                band = pl.ds(r * SUBLANES, SUBLANES)
                c, rest = divmod(r * SUBLANES, half_rows)
                part = pl.ds(rest, SUBLANES)
                left = jnp.where(first_tile, EMPTY, left_refs[c][s, l, part, :])
                joined = jnp.concatenate([left, own_refs[c][s, l, part, :]], axis=1)
                shifted_ref[l, k, band, :] = pltpu.roll(joined, shift, 1)[:, width:]

    cmap = cmap_ref[...]
    following = pltpu.roll(cmap, knot_count - 1, 1)
    delta = following - cmap
    tables = []
    for src in (cmap, delta):
        for c in range(4):
            for h in range(knot_count // LANES):
                row = src[c : c + 1, h * LANES : (h + 1) * LANES]
                tables.append(jnp.broadcast_to(row, (SUBLANES, LANES)))

    pieces = width // LANES

    def block(i, carry):
        r = i // pieces
        j = i % pieces
        band = pl.ds(pl.multiple_of(r * SUBLANES, SUBLANES), SUBLANES)
        cols = pl.ds(pl.multiple_of(j * LANES, LANES), LANES)
        depth_sum = jnp.zeros((SUBLANES, LANES), jnp.float32)
        image = [jnp.zeros((SUBLANES, LANES), jnp.float32) for _ in range(3)]
        for k in range(slabs):
            tau = None
            color = None
            for l in range(layers):
                cells = shifted_ref[l, k, band, cols]
                values = lookup(cells, tables, knot_count)
                absorb = jnp.where(cells < 100.0, values[3] * (6.0 / layers_overall), 0.0)
                through = jnp.exp(-absorb)
                opacity = 1.0 - through
                emit = [values[c] * opacity for c in range(3)]
                if tau is None:
                    color = emit
                    tau = absorb
                else:
                    fade = jnp.exp(-tau)
                    color = [color[c] + fade * emit[c] for c in range(3)]
                    tau = tau + absorb
            if k == 0:
                image = color
            else:
                fade = jnp.exp(-depth_sum)
                image = [image[c] + fade * color[c] for c in range(3)]
            depth_sum = depth_sum + tau
        for c in range(3):
            out_ref[c, band, cols] = image[c]
        out_ref[3, band, cols] = 1.0 - jnp.exp(-depth_sum)
        return carry

    lax.fori_loop(0, (rows // SUBLANES) * pieces, block, 0)


def shards(thermal_grid, colormap_samples, sheetgroup_viewer_sequence, occupied_lines, skew_offsets):
    layers, rows, width = thermal_grid.shape
    slabs = lax.axis_size("depth")
    regions = lax.axis_size("region")
    share = rows // slabs
    me = lax.axis_index("depth")
    halves = 2 if share % (2 * SUBLANES) == 0 else 1
    half = share // halves
    line = lax.broadcasted_iota(jnp.int32, (1, half, 1), 1)
    owns, lefts = [], []
    gate = None
    for c in range(halves):
        held = []
        for m in range(slabs):
            start = ((me - m) % slabs) * share + c * half
            piece = lax.dynamic_slice_in_dim(thermal_grid, start, half, axis=1)
            piece = jnp.where(start + line < occupied_lines[0, 0], piece, EMPTY)
            if gate is not None:
                piece = piece + gate
            if m > 0:
                piece = lax.ppermute(piece, "depth", [(i, (i - m) % slabs) for i in range(slabs)])
            held.append(piece)
        own = jnp.stack(held, axis=0)
        owns.append(own)
        gate = 0.0 * own[1:, 0, 0, 0].sum()
        lefts.append(lax.ppermute(own, "region", [(i, i + 1) for i in range(regions - 1)]))
    vmem = pltpu.VMEM
    smem = pltpu.SMEM
    placed = [pltpu.with_memory_space_constraint(x, vmem) for x in owns + lefts]
    return pl.pallas_call(
        render_kernel,
        out_shape=jax.ShapeDtypeStruct((4, share, width), jnp.float32),
        in_specs=[
            pl.BlockSpec(memory_space=smem),
            pl.BlockSpec(memory_space=smem),
        ]
        + [pl.BlockSpec(memory_space=vmem)] * (2 * halves + 1),
        out_specs=pl.BlockSpec(memory_space=vmem),
        scratch_shapes=[pltpu.VMEM((layers, slabs, share, width), jnp.float32)],
    )(sheetgroup_viewer_sequence, skew_offsets, *placed, colormap_samples)


def solution(mesh):
    in_specs = (P("depth", None, "region"), P(), P(), P("depth", "region"), P())
    out_specs = P(None, "depth", "region")
    return jax.shard_map(shards, mesh=mesh, in_specs=in_specs, out_specs=out_specs, check_vma=False)
```

```python
import functools

import jax
import jax.numpy as jnp
from jax import lax
from jax.experimental import pallas as pl
from jax.experimental.pallas import tpu as pltpu
from jax.sharding import PartitionSpec as P

EMPTY = 1.0e6
LANES = 128
SUBLANES = 8


def partner(i, m, n, sign=1):
    if n & (n - 1) == 0:
        return i ^ m
    return (i + sign * m) % n


def slot_of(s, me, n):
    if n & (n - 1) == 0:
        return s ^ me
    return (s - me + n) % n


def lookup(cells, tables, knot_count):
    scaled = jnp.clip((cells + 3.0) * ((knot_count - 1) / 6.0), 0.0, knot_count - 1.0)
    lower = jnp.minimum(jnp.floor(scaled), knot_count - 2.0)
    fraction = scaled - lower
    index = lower.astype(jnp.int32)
    upper_half = index >= LANES
    lane = jnp.where(upper_half, index - LANES, index)
    values = []
    for c in range(4):
        picked = []
        for base in (0, 8):
            low = jnp.take_along_axis(tables[base + 2 * c], lane, axis=1, mode="promise_in_bounds")
            high = jnp.take_along_axis(tables[base + 2 * c + 1], lane, axis=1, mode="promise_in_bounds")
            picked.append(jnp.where(upper_half, high, low))
        values.append(picked[0] + fraction * picked[1])
    return values


def render_kernel(seq_ref, skew_ref, *refs):
    halves = (len(refs) - 3) // 2
    own_refs, left_refs = refs[:halves], refs[halves : 2 * halves]
    cmap_ref, out_ref, shifted_ref = refs[2 * halves :]
    slabs, layers, half_rows, width = own_refs[0].shape
    rows = half_rows * halves
    layers_overall = layers * slabs
    knot_count = cmap_ref.shape[1]
    first_tile = lax.axis_index("region") == 0
    me = lax.axis_index("depth")
    skew = skew_ref[0]

    order = []
    for k in range(slabs):
        s = jnp.int32(0)
        for j in range(slabs):
            s = s + jnp.where(seq_ref[j] == k, j, 0)
        order.append(slot_of(s, me, slabs))

    for k in range(slabs):
        s = order[k]
        for l in range(layers):
            shift = ((k * layers + l) * skew) // layers_overall
            for r in range(rows // SUBLANES):
                band = pl.ds(r * SUBLANES, SUBLANES)
                c, rest = divmod(r * SUBLANES, half_rows)
                part = pl.ds(rest, SUBLANES)
                left = jnp.where(first_tile, EMPTY, left_refs[c][s, l, part, :])
                joined = jnp.concatenate([left, own_refs[c][s, l, part, :]], axis=1)
                shifted_ref[l, k, band, :] = pltpu.roll(joined, shift, 1)[:, width:]

    cmap = cmap_ref[...]
    following = pltpu.roll(cmap, knot_count - 1, 1)
    delta = following - cmap
    tables = []
    for src in (cmap, delta):
        for c in range(4):
            for h in range(knot_count // LANES):
                row = src[c : c + 1, h * LANES : (h + 1) * LANES]
                tables.append(jnp.broadcast_to(row, (SUBLANES, LANES)))

    pieces = width // LANES

    def block(i, carry):
        r = i // pieces
        j = i % pieces
        band = pl.ds(pl.multiple_of(r * SUBLANES, SUBLANES), SUBLANES)
        cols = pl.ds(pl.multiple_of(j * LANES, LANES), LANES)
        depth_sum = jnp.zeros((SUBLANES, LANES), jnp.float32)
        image = [jnp.zeros((SUBLANES, LANES), jnp.float32) for _ in range(3)]
        for k in range(slabs):
            tau = None
            color = None
            for l in range(layers):
                cells = shifted_ref[l, k, band, cols]
                values = lookup(cells, tables, knot_count)
                absorb = jnp.where(cells < 100.0, values[3] * (6.0 / layers_overall), 0.0)
                through = jnp.exp(-absorb)
                opacity = 1.0 - through
                emit = [values[c] * opacity for c in range(3)]
                if tau is None:
                    color = emit
                    tau = absorb
                else:
                    fade = jnp.exp(-tau)
                    color = [color[c] + fade * emit[c] for c in range(3)]
                    tau = tau + absorb
            if k == 0:
                image = color
            else:
                fade = jnp.exp(-depth_sum)
                image = [image[c] + fade * color[c] for c in range(3)]
            depth_sum = depth_sum + tau
        for c in range(3):
            out_ref[c, band, cols] = image[c]
        out_ref[3, band, cols] = 1.0 - jnp.exp(-depth_sum)
        return carry

    lax.fori_loop(0, (rows // SUBLANES) * pieces, block, 0)


def shards(thermal_grid, colormap_samples, sheetgroup_viewer_sequence, occupied_lines, skew_offsets):
    layers, rows, width = thermal_grid.shape
    slabs = lax.axis_size("depth")
    regions = lax.axis_size("region")
    share = rows // slabs
    me = lax.axis_index("depth")
    halves = 2 if share % (2 * SUBLANES) == 0 else 1
    half = share // halves
    line = lax.broadcasted_iota(jnp.int32, (1, half, 1), 1)
    owns, lefts = [], []
    for c in range(halves):
        held = []
        for m in range(slabs):
            start = partner(me, m, slabs, -1) * share + c * half
            piece = lax.dynamic_slice_in_dim(thermal_grid, start, half, axis=1)
            piece = jnp.where(start + line < occupied_lines[0, 0], piece, EMPTY)
            if m > 0:
                route = [(i, partner(i, m, slabs, -1)) for i in range(slabs)]
                piece = lax.ppermute(piece, "depth", route)
            held.append(piece)
        own = jnp.stack(held, axis=0)
        owns.append(own)
        lefts.append(lax.ppermute(own, "region", [(i, i + 1) for i in range(regions - 1)]))
    vmem = pltpu.VMEM
    smem = pltpu.SMEM
    placed = [pltpu.with_memory_space_constraint(x, vmem) for x in owns + lefts]
    return pl.pallas_call(
        render_kernel,
        out_shape=jax.ShapeDtypeStruct((4, share, width), jnp.float32),
        in_specs=[
            pl.BlockSpec(memory_space=smem),
            pl.BlockSpec(memory_space=smem),
        ]
        + [pl.BlockSpec(memory_space=vmem)] * (2 * halves + 1),
        out_specs=pl.BlockSpec(memory_space=vmem),
        scratch_shapes=[pltpu.VMEM((layers, slabs, share, width), jnp.float32)],
    )(sheetgroup_viewer_sequence, skew_offsets, *placed, colormap_samples)


def solution(mesh):
    in_specs = (P("depth", None, "region"), P(), P(), P("depth", "region"), P())
    out_specs = P(None, "depth", "region")
    return jax.shard_map(shards, mesh=mesh, in_specs=in_specs, out_specs=out_specs, check_vma=False)
```

```python
import functools

import jax
import jax.numpy as jnp
from jax import lax
from jax.experimental import pallas as pl
from jax.experimental.pallas import tpu as pltpu
from jax.sharding import PartitionSpec as P

EMPTY = 1.0e6
LANES = 128
SUBLANES = 8


def partner(i, m, n, sign=1):
    if n & (n - 1) == 0:
        return i ^ m
    return (i + sign * m) % n


def slot_of(s, me, n):
    if n & (n - 1) == 0:
        return s ^ me
    return (s - me + n) % n


def lookup(cells, tables, knot_count):
    scaled = jnp.clip((cells + 3.0) * ((knot_count - 1) / 6.0), 0.0, knot_count - 1.0)
    lower = jnp.minimum(jnp.floor(scaled), knot_count - 2.0)
    fraction = scaled - lower
    index = lower.astype(jnp.int32)
    upper_half = index >= LANES
    lane = jnp.where(upper_half, index - LANES, index)
    values = []
    for c in range(4):
        picked = []
        for base in (0, 8):
            low = jnp.take_along_axis(tables[base + 2 * c], lane, axis=1, mode="promise_in_bounds")
            high = jnp.take_along_axis(tables[base + 2 * c + 1], lane, axis=1, mode="promise_in_bounds")
            picked.append(jnp.where(upper_half, high, low))
        values.append(picked[0] + fraction * picked[1])
    return values


def render_kernel(seq_ref, skew_ref, *refs):
    halves = (len(refs) - 4) // 2
    own_refs, left_refs = refs[:halves], refs[halves : 2 * halves]
    left_first_ref, cmap_ref, out_ref, shifted_ref = refs[2 * halves :]
    slabs, layers, half_rows, width = own_refs[0].shape
    rows = half_rows * halves
    layers_overall = layers * slabs
    knot_count = cmap_ref.shape[1]
    first_tile = lax.axis_index("region") == 0
    me = lax.axis_index("depth")
    skew = skew_ref[0]

    order = []
    for k in range(slabs):
        s = jnp.int32(0)
        for j in range(slabs):
            s = s + jnp.where(seq_ref[j] == k, j, 0)
        order.append(slot_of(s, me, slabs))

    for k in range(slabs):
        s = order[k]
        for l in range(layers):
            shift = ((k * layers + l) * skew) // layers_overall
            for r in range(rows // SUBLANES):
                band = pl.ds(r * SUBLANES, SUBLANES)
                c, rest = divmod(r * SUBLANES, half_rows)
                part = pl.ds(rest, SUBLANES)
                left = jnp.where(
                    s == 0,
                    left_first_ref[l, band, :],
                    left_refs[c][jnp.maximum(s - 1, 0), l, part, :],
                )
                left = jnp.where(first_tile, EMPTY, left)
                joined = jnp.concatenate([left, own_refs[c][s, l, part, :]], axis=1)
                shifted_ref[l, k, band, :] = pltpu.roll(joined, shift, 1)[:, width:]

    cmap = cmap_ref[...]
    following = pltpu.roll(cmap, knot_count - 1, 1)
    delta = following - cmap
    tables = []
    for src in (cmap, delta):
        for c in range(4):
            for h in range(knot_count // LANES):
                row = src[c : c + 1, h * LANES : (h + 1) * LANES]
                tables.append(jnp.broadcast_to(row, (SUBLANES, LANES)))

    pieces = width // LANES

    def block(i, carry):
        r = i // pieces
        j = i % pieces
        band = pl.ds(pl.multiple_of(r * SUBLANES, SUBLANES), SUBLANES)
        cols = pl.ds(pl.multiple_of(j * LANES, LANES), LANES)
        depth_sum = jnp.zeros((SUBLANES, LANES), jnp.float32)
        image = [jnp.zeros((SUBLANES, LANES), jnp.float32) for _ in range(3)]
        for k in range(slabs):
            tau = None
            color = None
            for l in range(layers):
                cells = shifted_ref[l, k, band, cols]
                values = lookup(cells, tables, knot_count)
                absorb = jnp.where(cells < 100.0, values[3] * (6.0 / layers_overall), 0.0)
                through = jnp.exp(-absorb)
                opacity = 1.0 - through
                emit = [values[c] * opacity for c in range(3)]
                if tau is None:
                    color = emit
                    tau = absorb
                else:
                    fade = jnp.exp(-tau)
                    color = [color[c] + fade * emit[c] for c in range(3)]
                    tau = tau + absorb
            if k == 0:
                image = color
            else:
                fade = jnp.exp(-depth_sum)
                image = [image[c] + fade * color[c] for c in range(3)]
            depth_sum = depth_sum + tau
        for c in range(3):
            out_ref[c, band, cols] = image[c]
        out_ref[3, band, cols] = 1.0 - jnp.exp(-depth_sum)
        return carry

    lax.fori_loop(0, (rows // SUBLANES) * pieces, block, 0)


def shards(thermal_grid, colormap_samples, sheetgroup_viewer_sequence, occupied_lines, skew_offsets):
    layers, rows, width = thermal_grid.shape
    slabs = lax.axis_size("depth")
    regions = lax.axis_size("region")
    share = rows // slabs
    me = lax.axis_index("depth")
    halves = 2 if share % (2 * SUBLANES) == 0 else 1
    half = share // halves
    line = lax.broadcasted_iota(jnp.int32, (1, half, 1), 1)
    to_right = [(i, i + 1) for i in range(regions - 1)]
    own_rows = me * share
    first = lax.dynamic_slice_in_dim(thermal_grid, own_rows, share, axis=1)
    first = jnp.where(own_rows + lax.broadcasted_iota(jnp.int32, (1, share, 1), 1) < occupied_lines[0, 0], first, EMPTY)
    left_first = lax.ppermute(first, "region", to_right)
    gate = 0.0 * left_first[0, 0, 0]
    owns, lefts = [], []
    for c in range(halves):
        held = [first[:, c * half : (c + 1) * half]]
        for m in range(1, slabs):
            start = partner(me, m, slabs, -1) * share + c * half
            piece = lax.dynamic_slice_in_dim(thermal_grid, start, half, axis=1)
            piece = jnp.where(start + line < occupied_lines[0, 0], piece, EMPTY)
            route = [(i, partner(i, m, slabs, -1)) for i in range(slabs)]
            held.append(lax.ppermute(piece, "depth", route))
        owns.append(jnp.stack(held, axis=0))
        lefts.append(lax.ppermute(jnp.stack(held[1:], axis=0) + gate, "region", to_right))
    vmem = pltpu.VMEM
    smem = pltpu.SMEM
    placed = [pltpu.with_memory_space_constraint(x, vmem) for x in owns + lefts + [left_first]]
    return pl.pallas_call(
        render_kernel,
        out_shape=jax.ShapeDtypeStruct((4, share, width), jnp.float32),
        in_specs=[
            pl.BlockSpec(memory_space=smem),
            pl.BlockSpec(memory_space=smem),
        ]
        + [pl.BlockSpec(memory_space=vmem)] * (2 * halves + 2),
        out_specs=pl.BlockSpec(memory_space=vmem),
        scratch_shapes=[pltpu.VMEM((layers, slabs, share, width), jnp.float32)],
    )(sheetgroup_viewer_sequence, skew_offsets, *placed, colormap_samples)


def solution(mesh):
    in_specs = (P("depth", None, "region"), P(), P(), P("depth", "region"), P())
    out_specs = P(None, "depth", "region")
    return jax.shard_map(shards, mesh=mesh, in_specs=in_specs, out_specs=out_specs, check_vma=False)
```

```python
import functools

import jax
import jax.numpy as jnp
from jax import lax
from jax.experimental import pallas as pl
from jax.experimental.pallas import tpu as pltpu
from jax.sharding import PartitionSpec as P

EMPTY = 1.0e6
LANES = 128
SUBLANES = 8


def partner(i, m, n, sign=1):
    if n & (n - 1) == 0:
        return i ^ m
    return (i + sign * m) % n


def slot_of(s, me, n):
    if n & (n - 1) == 0:
        return s ^ me
    return (s - me + n) % n


def lookup(cells, tables, knot_count):
    scaled = jnp.clip((cells + 3.0) * ((knot_count - 1) / 6.0), 0.0, knot_count - 1.0)
    lower = jnp.minimum(jnp.floor(scaled), knot_count - 2.0)
    fraction = scaled - lower
    index = lower.astype(jnp.int32)
    upper_half = index >= LANES
    lane = jnp.where(upper_half, index - LANES, index)
    values = []
    for c in range(4):
        picked = []
        for base in (0, 8):
            low = jnp.take_along_axis(tables[base + 2 * c], lane, axis=1, mode="promise_in_bounds")
            high = jnp.take_along_axis(tables[base + 2 * c + 1], lane, axis=1, mode="promise_in_bounds")
            picked.append(jnp.where(upper_half, high, low))
        values.append(picked[0] + fraction * picked[1])
    return values


def render_kernel(seq_ref, skew_ref, *refs):
    halves = (len(refs) - 3) // 2
    own_refs, left_refs = refs[:halves], refs[halves : 2 * halves]
    cmap_ref, out_ref, shifted_ref = refs[2 * halves :]
    slabs, layers, _, width = own_refs[0].shape
    bounds = [0]
    for ref in own_refs:
        bounds.append(bounds[-1] + ref.shape[2])
    rows = bounds[-1]
    layers_overall = layers * slabs
    knot_count = cmap_ref.shape[1]
    first_tile = lax.axis_index("region") == 0
    me = lax.axis_index("depth")
    skew = skew_ref[0]

    order = []
    for k in range(slabs):
        s = jnp.int32(0)
        for j in range(slabs):
            s = s + jnp.where(seq_ref[j] == k, j, 0)
        order.append(slot_of(s, me, slabs))

    for k in range(slabs):
        s = order[k]
        for l in range(layers):
            shift = ((k * layers + l) * skew) // layers_overall
            for r in range(rows // SUBLANES):
                band = pl.ds(r * SUBLANES, SUBLANES)
                c = max(i for i in range(halves) if bounds[i] <= r * SUBLANES)
                rest = r * SUBLANES - bounds[c]
                part = pl.ds(rest, SUBLANES)
                left = jnp.where(first_tile, EMPTY, left_refs[c][s, l, part, :])
                joined = jnp.concatenate([left, own_refs[c][s, l, part, :]], axis=1)
                shifted_ref[l, k, band, :] = pltpu.roll(joined, shift, 1)[:, width:]

    cmap = cmap_ref[...]
    following = pltpu.roll(cmap, knot_count - 1, 1)
    delta = following - cmap
    tables = []
    for src in (cmap, delta):
        for c in range(4):
            for h in range(knot_count // LANES):
                row = src[c : c + 1, h * LANES : (h + 1) * LANES]
                tables.append(jnp.broadcast_to(row, (SUBLANES, LANES)))

    pieces = width // LANES

    def block(i, carry):
        r = i // pieces
        j = i % pieces
        band = pl.ds(pl.multiple_of(r * SUBLANES, SUBLANES), SUBLANES)
        cols = pl.ds(pl.multiple_of(j * LANES, LANES), LANES)
        depth_sum = jnp.zeros((SUBLANES, LANES), jnp.float32)
        image = [jnp.zeros((SUBLANES, LANES), jnp.float32) for _ in range(3)]
        for k in range(slabs):
            tau = None
            color = None
            for l in range(layers):
                cells = shifted_ref[l, k, band, cols]
                values = lookup(cells, tables, knot_count)
                absorb = jnp.where(cells < 100.0, values[3] * (6.0 / layers_overall), 0.0)
                through = jnp.exp(-absorb)
                opacity = 1.0 - through
                emit = [values[c] * opacity for c in range(3)]
                if tau is None:
                    color = emit
                    tau = absorb
                else:
                    fade = jnp.exp(-tau)
                    color = [color[c] + fade * emit[c] for c in range(3)]
                    tau = tau + absorb
            if k == 0:
                image = color
            else:
                fade = jnp.exp(-depth_sum)
                image = [image[c] + fade * color[c] for c in range(3)]
            depth_sum = depth_sum + tau
        for c in range(3):
            out_ref[c, band, cols] = image[c]
        out_ref[3, band, cols] = 1.0 - jnp.exp(-depth_sum)
        return carry

    lax.fori_loop(0, (rows // SUBLANES) * pieces, block, 0)


def shards(thermal_grid, colormap_samples, sheetgroup_viewer_sequence, occupied_lines, skew_offsets):
    layers, rows, width = thermal_grid.shape
    slabs = lax.axis_size("depth")
    regions = lax.axis_size("region")
    share = rows // slabs
    me = lax.axis_index("depth")
    if share % (4 * SUBLANES) == 0:
        chunks = [share * 3 // 4, share // 4]
    else:
        chunks = [share]
    owns, lefts = [], []
    for c, half in enumerate(chunks):
        line = lax.broadcasted_iota(jnp.int32, (1, half, 1), 1)
        held = []
        for m in range(slabs):
            start = partner(me, m, slabs, -1) * share + sum(chunks[:c])
            piece = lax.dynamic_slice_in_dim(thermal_grid, start, half, axis=1)
            piece = jnp.where(start + line < occupied_lines[0, 0], piece, EMPTY)
            if m > 0:
                route = [(i, partner(i, m, slabs, -1)) for i in range(slabs)]
                piece = lax.ppermute(piece, "depth", route)
            held.append(piece)
        own = jnp.stack(held, axis=0)
        owns.append(own)
        lefts.append(lax.ppermute(own, "region", [(i, i + 1) for i in range(regions - 1)]))
    vmem = pltpu.VMEM
    smem = pltpu.SMEM
    placed = [pltpu.with_memory_space_constraint(x, vmem) for x in owns + lefts]
    return pl.pallas_call(
        render_kernel,
        out_shape=jax.ShapeDtypeStruct((4, share, width), jnp.float32),
        in_specs=[
            pl.BlockSpec(memory_space=smem),
            pl.BlockSpec(memory_space=smem),
        ]
        + [pl.BlockSpec(memory_space=vmem)] * (2 * len(chunks) + 1),
        out_specs=pl.BlockSpec(memory_space=vmem),
        scratch_shapes=[pltpu.VMEM((layers, slabs, share, width), jnp.float32)],
    )(sheetgroup_viewer_sequence, skew_offsets, *placed, colormap_samples)


def solution(mesh):
    in_specs = (P("depth", None, "region"), P(), P(), P("depth", "region"), P())
    out_specs = P(None, "depth", "region")
    return jax.shard_map(shards, mesh=mesh, in_specs=in_specs, out_specs=out_specs, check_vma=False)
```

```python
import functools

import jax
import jax.numpy as jnp
from jax import lax
from jax.experimental import pallas as pl
from jax.experimental.pallas import tpu as pltpu
from jax.sharding import PartitionSpec as P

EMPTY = 1.0e6
LANES = 128
SUBLANES = 8


def partner(i, m, n, sign=1):
    if n & (n - 1) == 0:
        return i ^ m
    return (i + sign * m) % n


def slot_of(s, me, n):
    if n & (n - 1) == 0:
        return s ^ me
    return (s - me + n) % n


def lookup(cells, tables, knot_count):
    scaled = jnp.clip((cells + 3.0) * ((knot_count - 1) / 6.0), 0.0, knot_count - 1.0)
    lower = jnp.minimum(jnp.floor(scaled), knot_count - 2.0)
    fraction = scaled - lower
    index = lower.astype(jnp.int32)
    upper_half = index >= LANES
    lane = jnp.where(upper_half, index - LANES, index)
    values = []
    for c in range(4):
        picked = []
        for base in (0, 8):
            low = jnp.take_along_axis(tables[base + 2 * c], lane, axis=1, mode="promise_in_bounds")
            high = jnp.take_along_axis(tables[base + 2 * c + 1], lane, axis=1, mode="promise_in_bounds")
            picked.append(jnp.where(upper_half, high, low))
        values.append(picked[0] + fraction * picked[1])
    return values


def render_kernel(seq_ref, skew_ref, *refs):
    halves = (len(refs) - 3) // 2
    own_refs, left_refs = refs[:halves], refs[halves : 2 * halves]
    cmap_ref, out_ref, shifted_ref = refs[2 * halves :]
    slabs, layers, half_rows, width = own_refs[0].shape
    rows = half_rows * halves
    layers_overall = layers * slabs
    knot_count = cmap_ref.shape[1]
    first_tile = lax.axis_index("region") == 0
    me = lax.axis_index("depth")
    skew = skew_ref[0]

    order = []
    for k in range(slabs):
        s = jnp.int32(0)
        for j in range(slabs):
            s = s + jnp.where(seq_ref[j] == k, j, 0)
        order.append(slot_of(s, me, slabs))

    for k in range(slabs):
        s = order[k]
        for l in range(layers):
            shift = ((k * layers + l) * skew) // layers_overall
            for r in range(rows // SUBLANES):
                band = pl.ds(r * SUBLANES, SUBLANES)
                c, rest = divmod(r * SUBLANES, half_rows)
                part = pl.ds(rest, SUBLANES)
                left = jnp.where(first_tile, EMPTY, left_refs[c][s, l, part, :])
                joined = jnp.concatenate([left, own_refs[c][s, l, part, :]], axis=1)
                shifted_ref[l, k, band, :] = pltpu.roll(joined, shift, 1)[:, width:]

    cmap = cmap_ref[...]
    following = pltpu.roll(cmap, knot_count - 1, 1)
    delta = following - cmap
    tables = []
    for src in (cmap, delta):
        for c in range(4):
            for h in range(knot_count // LANES):
                row = src[c : c + 1, h * LANES : (h + 1) * LANES]
                tables.append(jnp.broadcast_to(row, (SUBLANES, LANES)))

    pieces = width // LANES

    def block(i, carry):
        r = i // pieces
        j = i % pieces
        band = pl.ds(pl.multiple_of(r * SUBLANES, SUBLANES), SUBLANES)
        cols = pl.ds(pl.multiple_of(j * LANES, LANES), LANES)
        depth_sum = jnp.zeros((SUBLANES, LANES), jnp.float32)
        image = [jnp.zeros((SUBLANES, LANES), jnp.float32) for _ in range(3)]
        for k in range(slabs):
            tau = None
            color = None
            for l in range(layers):
                cells = shifted_ref[l, k, band, cols]
                values = lookup(cells, tables, knot_count)
                absorb = jnp.where(cells < 100.0, values[3] * (6.0 / layers_overall), 0.0)
                through = jnp.exp(-absorb)
                opacity = 1.0 - through
                emit = [values[c] * opacity for c in range(3)]
                if tau is None:
                    color = emit
                    tau = absorb
                else:
                    fade = jnp.exp(-tau)
                    color = [color[c] + fade * emit[c] for c in range(3)]
                    tau = tau + absorb
            if k == 0:
                image = color
            else:
                fade = jnp.exp(-depth_sum)
                image = [image[c] + fade * color[c] for c in range(3)]
            depth_sum = depth_sum + tau
        for c in range(3):
            out_ref[c, band, cols] = image[c]
        out_ref[3, band, cols] = 1.0 - jnp.exp(-depth_sum)
        return carry

    lax.fori_loop(0, (rows // SUBLANES) * pieces, block, 0)


def shards(thermal_grid, colormap_samples, sheetgroup_viewer_sequence, occupied_lines, skew_offsets):
    layers, rows, width = thermal_grid.shape
    slabs = lax.axis_size("depth")
    regions = lax.axis_size("region")
    share = rows // slabs
    me = lax.axis_index("depth")
    halves = 2 if share % (2 * SUBLANES) == 0 else 1
    half = share // halves
    line = lax.broadcasted_iota(jnp.int32, (1, half, 1), 1)
    owns, lefts = [], []
    for c in range(halves):
        held = []
        for m in range(slabs):
            start = partner(me, m, slabs, -1) * share + c * half
            piece = lax.dynamic_slice_in_dim(thermal_grid, start, half, axis=1)
            piece = jnp.where(start + line < occupied_lines[0, 0], piece, EMPTY)
            if m > 0:
                route = [(i, partner(i, m, slabs, -1)) for i in range(slabs)]
                piece = lax.ppermute(piece, "depth", route)
            held.append(piece)
        own = jnp.stack(held, axis=0)
        owns.append(own)
        lefts.append(lax.ppermute(own, "region", [(i, i + 1) for i in range(regions - 1)]))
    vmem = pltpu.VMEM
    smem = pltpu.SMEM
    images = []
    for own, left in zip(owns, lefts):
        placed = [pltpu.with_memory_space_constraint(x, vmem) for x in (own, left)]
        images.append(
            pl.pallas_call(
                render_kernel,
                out_shape=jax.ShapeDtypeStruct((4, half, width), jnp.float32),
                in_specs=[pl.BlockSpec(memory_space=smem)] * 2 + [pl.BlockSpec(memory_space=vmem)] * 3,
                out_specs=pl.BlockSpec(memory_space=vmem),
                scratch_shapes=[pltpu.VMEM((layers, slabs, half, width), jnp.float32)],
            )(sheetgroup_viewer_sequence, skew_offsets, *placed, colormap_samples)
        )
    return jnp.concatenate(images, axis=1) if len(images) > 1 else images[0]


def solution(mesh):
    in_specs = (P("depth", None, "region"), P(), P(), P("depth", "region"), P())
    out_specs = P(None, "depth", "region")
    return jax.shard_map(shards, mesh=mesh, in_specs=in_specs, out_specs=out_specs, check_vma=False)
```

```python
import functools

import jax
import jax.numpy as jnp
from jax import lax
from jax.experimental import pallas as pl
from jax.experimental.pallas import tpu as pltpu
from jax.sharding import PartitionSpec as P

EMPTY = 1.0e6
LANES = 128
SUBLANES = 8


def partner(i, m, n, sign=1):
    if n & (n - 1) == 0:
        return i ^ m
    return (i + sign * m) % n


def slot_of(s, me, n):
    if n & (n - 1) == 0:
        return s ^ me
    return (s - me + n) % n


def lookup(cells, tables, knot_count):
    scaled = jnp.clip((cells + 3.0) * ((knot_count - 1) / 6.0), 0.0, knot_count - 1.0)
    lower = jnp.minimum(jnp.floor(scaled), knot_count - 2.0)
    fraction = scaled - lower
    index = lower.astype(jnp.int32)
    upper_half = index >= LANES
    lane = jnp.where(upper_half, index - LANES, index)
    values = []
    for c in range(4):
        picked = []
        for base in (0, 8):
            low = jnp.take_along_axis(tables[base + 2 * c], lane, axis=1, mode="promise_in_bounds")
            high = jnp.take_along_axis(tables[base + 2 * c + 1], lane, axis=1, mode="promise_in_bounds")
            picked.append(jnp.where(upper_half, high, low))
        values.append(picked[0] + fraction * picked[1])
    return values


def render_kernel(first_row, seq_ref, skew_ref, own_ref, left_ref, cmap_ref, *refs):
    out_hbm, shifted_ref, out_ref, sem = refs[-4:]
    halves = 1
    own_refs, left_refs = (own_ref,), (left_ref,)
    slabs, layers, half_rows, width = own_refs[0].shape
    rows = half_rows * halves
    layers_overall = layers * slabs
    knot_count = cmap_ref.shape[1]
    first_tile = lax.axis_index("region") == 0
    me = lax.axis_index("depth")
    skew = skew_ref[0]

    order = []
    for k in range(slabs):
        s = jnp.int32(0)
        for j in range(slabs):
            s = s + jnp.where(seq_ref[j] == k, j, 0)
        order.append(slot_of(s, me, slabs))

    for k in range(slabs):
        s = order[k]
        for l in range(layers):
            shift = ((k * layers + l) * skew) // layers_overall
            for r in range(rows // SUBLANES):
                band = pl.ds(r * SUBLANES, SUBLANES)
                c, rest = divmod(r * SUBLANES, half_rows)
                part = pl.ds(rest, SUBLANES)
                left = jnp.where(first_tile, EMPTY, left_refs[c][s, l, part, :])
                joined = jnp.concatenate([left, own_refs[c][s, l, part, :]], axis=1)
                shifted_ref[l, k, band, :] = pltpu.roll(joined, shift, 1)[:, width:]

    cmap = cmap_ref[...]
    following = pltpu.roll(cmap, knot_count - 1, 1)
    delta = following - cmap
    tables = []
    for src in (cmap, delta):
        for c in range(4):
            for h in range(knot_count // LANES):
                row = src[c : c + 1, h * LANES : (h + 1) * LANES]
                tables.append(jnp.broadcast_to(row, (SUBLANES, LANES)))

    pieces = width // LANES

    def block(i, carry):
        r = i // pieces
        j = i % pieces
        band = pl.ds(pl.multiple_of(r * SUBLANES, SUBLANES), SUBLANES)
        cols = pl.ds(pl.multiple_of(j * LANES, LANES), LANES)
        depth_sum = jnp.zeros((SUBLANES, LANES), jnp.float32)
        image = [jnp.zeros((SUBLANES, LANES), jnp.float32) for _ in range(3)]
        for k in range(slabs):
            tau = None
            color = None
            for l in range(layers):
                cells = shifted_ref[l, k, band, cols]
                values = lookup(cells, tables, knot_count)
                absorb = jnp.where(cells < 100.0, values[3] * (6.0 / layers_overall), 0.0)
                through = jnp.exp(-absorb)
                opacity = 1.0 - through
                emit = [values[c] * opacity for c in range(3)]
                if tau is None:
                    color = emit
                    tau = absorb
                else:
                    fade = jnp.exp(-tau)
                    color = [color[c] + fade * emit[c] for c in range(3)]
                    tau = tau + absorb
            if k == 0:
                image = color
            else:
                fade = jnp.exp(-depth_sum)
                image = [image[c] + fade * color[c] for c in range(3)]
            depth_sum = depth_sum + tau
        for c in range(3):
            out_ref[c, band, cols] = image[c]
        out_ref[3, band, cols] = 1.0 - jnp.exp(-depth_sum)
        return carry

    lax.fori_loop(0, (rows // SUBLANES) * pieces, block, 0)
    copy = pltpu.make_async_copy(out_ref, out_hbm.at[:, pl.ds(first_row, rows), :], sem)
    copy.start()
    copy.wait()


def shards(thermal_grid, colormap_samples, sheetgroup_viewer_sequence, occupied_lines, skew_offsets):
    layers, rows, width = thermal_grid.shape
    slabs = lax.axis_size("depth")
    regions = lax.axis_size("region")
    share = rows // slabs
    me = lax.axis_index("depth")
    halves = 2 if share % (2 * SUBLANES) == 0 else 1
    half = share // halves
    line = lax.broadcasted_iota(jnp.int32, (1, half, 1), 1)
    owns, lefts = [], []
    for c in range(halves):
        held = []
        for m in range(slabs):
            start = partner(me, m, slabs, -1) * share + c * half
            piece = lax.dynamic_slice_in_dim(thermal_grid, start, half, axis=1)
            piece = jnp.where(start + line < occupied_lines[0, 0], piece, EMPTY)
            if m > 0:
                route = [(i, partner(i, m, slabs, -1)) for i in range(slabs)]
                piece = lax.ppermute(piece, "depth", route)
            held.append(piece)
        own = jnp.stack(held, axis=0)
        owns.append(own)
        lefts.append(lax.ppermute(own, "region", [(i, i + 1) for i in range(regions - 1)]))
    vmem = pltpu.VMEM
    smem = pltpu.SMEM
    image = None
    for c, (own, left) in enumerate(zip(owns, lefts)):
        placed = [pltpu.with_memory_space_constraint(x, vmem) for x in (own, left)]
        extra = [] if image is None else [image]
        image = pl.pallas_call(
            functools.partial(render_kernel, c * half),
            out_shape=jax.ShapeDtypeStruct((4, share, width), jnp.float32),
            in_specs=[pl.BlockSpec(memory_space=smem)] * 2
            + [pl.BlockSpec(memory_space=vmem)] * 3
            + [pl.BlockSpec(memory_space=pl.ANY)] * len(extra),
            out_specs=pl.BlockSpec(memory_space=pl.ANY),
            scratch_shapes=[
                pltpu.VMEM((layers, slabs, half, width), jnp.float32),
                pltpu.VMEM((4, half, width), jnp.float32),
                pltpu.SemaphoreType.DMA(()),
            ],
            input_output_aliases={5: 0} if extra else {},
        )(sheetgroup_viewer_sequence, skew_offsets, *placed, colormap_samples, *extra)
    return image


def solution(mesh):
    in_specs = (P("depth", None, "region"), P(), P(), P("depth", "region"), P())
    out_specs = P(None, "depth", "region")
    return jax.shard_map(shards, mesh=mesh, in_specs=in_specs, out_specs=out_specs, check_vma=False)
```

```python
import functools

import jax
import jax.numpy as jnp
from jax import lax
from jax.experimental import pallas as pl
from jax.experimental.pallas import tpu as pltpu
from jax.sharding import PartitionSpec as P

EMPTY = 1.0e6
LANES = 128
SUBLANES = 8


def butterfly(n):
    return n & (n - 1) == 0


def slot_of(s, me, n):
    if butterfly(n):
        return s
    return (s - me + n) % n


def lookup(cells, tables, knot_count):
    scaled = jnp.clip((cells + 3.0) * ((knot_count - 1) / 6.0), 0.0, knot_count - 1.0)
    lower = jnp.minimum(jnp.floor(scaled), knot_count - 2.0)
    fraction = scaled - lower
    index = lower.astype(jnp.int32)
    upper_half = index >= LANES
    lane = jnp.where(upper_half, index - LANES, index)
    values = []
    for c in range(4):
        picked = []
        for base in (0, 8):
            low = jnp.take_along_axis(tables[base + 2 * c], lane, axis=1, mode="promise_in_bounds")
            high = jnp.take_along_axis(tables[base + 2 * c + 1], lane, axis=1, mode="promise_in_bounds")
            picked.append(jnp.where(upper_half, high, low))
        values.append(picked[0] + fraction * picked[1])
    return values


def render_kernel(first_row, seq_ref, skew_ref, own_ref, left_ref, cmap_ref, *refs):
    out_hbm, shifted_ref, out_ref, sem = refs[-4:]
    halves = 1
    own_refs, left_refs = (own_ref,), (left_ref,)
    slabs, layers, half_rows, width = own_refs[0].shape
    rows = half_rows * halves
    layers_overall = layers * slabs
    knot_count = cmap_ref.shape[1]
    first_tile = lax.axis_index("region") == 0
    me = lax.axis_index("depth")
    skew = skew_ref[0]

    order = []
    for k in range(slabs):
        s = jnp.int32(0)
        for j in range(slabs):
            s = s + jnp.where(seq_ref[j] == k, j, 0)
        order.append(slot_of(s, me, slabs))

    for k in range(slabs):
        s = order[k]
        for l in range(layers):
            shift = ((k * layers + l) * skew) // layers_overall
            for r in range(rows // SUBLANES):
                band = pl.ds(r * SUBLANES, SUBLANES)
                c, rest = divmod(r * SUBLANES, half_rows)
                part = pl.ds(rest, SUBLANES)
                left = jnp.where(first_tile, EMPTY, left_refs[c][s, l, part, :])
                joined = jnp.concatenate([left, own_refs[c][s, l, part, :]], axis=1)
                shifted_ref[l, k, band, :] = pltpu.roll(joined, shift, 1)[:, width:]

    cmap = cmap_ref[...]
    following = pltpu.roll(cmap, knot_count - 1, 1)
    delta = following - cmap
    tables = []
    for src in (cmap, delta):
        for c in range(4):
            for h in range(knot_count // LANES):
                row = src[c : c + 1, h * LANES : (h + 1) * LANES]
                tables.append(jnp.broadcast_to(row, (SUBLANES, LANES)))

    pieces = width // LANES

    def block(i, carry):
        r = i // pieces
        j = i % pieces
        band = pl.ds(pl.multiple_of(r * SUBLANES, SUBLANES), SUBLANES)
        cols = pl.ds(pl.multiple_of(j * LANES, LANES), LANES)
        depth_sum = jnp.zeros((SUBLANES, LANES), jnp.float32)
        image = [jnp.zeros((SUBLANES, LANES), jnp.float32) for _ in range(3)]
        for k in range(slabs):
            tau = None
            color = None
            for l in range(layers):
                cells = shifted_ref[l, k, band, cols]
                values = lookup(cells, tables, knot_count)
                absorb = jnp.where(cells < 100.0, values[3] * (6.0 / layers_overall), 0.0)
                through = jnp.exp(-absorb)
                opacity = 1.0 - through
                emit = [values[c] * opacity for c in range(3)]
                if tau is None:
                    color = emit
                    tau = absorb
                else:
                    fade = jnp.exp(-tau)
                    color = [color[c] + fade * emit[c] for c in range(3)]
                    tau = tau + absorb
            if k == 0:
                image = color
            else:
                fade = jnp.exp(-depth_sum)
                image = [image[c] + fade * color[c] for c in range(3)]
            depth_sum = depth_sum + tau
        for c in range(3):
            out_ref[c, band, cols] = image[c]
        out_ref[3, band, cols] = 1.0 - jnp.exp(-depth_sum)
        return carry

    lax.fori_loop(0, (rows // SUBLANES) * pieces, block, 0)
    copy = pltpu.make_async_copy(out_ref, out_hbm.at[:, pl.ds(first_row, rows), :], sem)
    copy.start()
    copy.wait()


def shards(thermal_grid, colormap_samples, sheetgroup_viewer_sequence, occupied_lines, skew_offsets):
    layers, rows, width = thermal_grid.shape
    slabs = lax.axis_size("depth")
    regions = lax.axis_size("region")
    share = rows // slabs
    me = lax.axis_index("depth")
    halves = 2 if share % (2 * SUBLANES) == 0 else 1
    chunks = [share // halves] * halves
    owns, lefts = [], []
    start = 0
    for half in chunks:
        if butterfly(slabs):
            rows_here = lax.broadcasted_iota(jnp.int32, (1, slabs, half, 1), 1) * share
            rows_here = rows_here + lax.broadcasted_iota(jnp.int32, (1, slabs, half, 1), 2) + start
            cut = thermal_grid.reshape(layers, slabs, share, width)[:, :, start : start + half]
            cut = jnp.where(rows_here < occupied_lines[0, 0], cut, EMPTY)
            held = jnp.transpose(cut, (1, 0, 2, 3))
            for b in reversed(range(slabs.bit_length() - 1)):
                away = 1 - (me >> b) % 2
                split = held.reshape(slabs >> (b + 1), 2, 1 << b, layers, half, width)
                sent = lax.dynamic_index_in_dim(split, away, axis=1, keepdims=False)
                route = [(i, i ^ (1 << b)) for i in range(slabs)]
                got = lax.ppermute(sent, "depth", route)
                side = lax.broadcasted_iota(jnp.int32, (1, 2, 1, 1, 1, 1), 1)
                split = jnp.where(side == away, got[:, None], split)
                held = split.reshape(slabs, layers, half, width)
            own = held
        else:
            line = lax.broadcasted_iota(jnp.int32, (1, half, 1), 1)
            pieces = []
            for m in range(slabs):
                first = ((me - m) % slabs) * share + start
                piece = lax.dynamic_slice_in_dim(thermal_grid, first, half, axis=1)
                piece = jnp.where(first + line < occupied_lines[0, 0], piece, EMPTY)
                if m > 0:
                    route = [(i, (i - m) % slabs) for i in range(slabs)]
                    piece = lax.ppermute(piece, "depth", route)
                pieces.append(piece)
            own = jnp.stack(pieces, axis=0)
        owns.append(own)
        lefts.append(lax.ppermute(own, "region", [(i, i + 1) for i in range(regions - 1)]))
        start += half
    vmem = pltpu.VMEM
    smem = pltpu.SMEM
    image = None
    for c, (own, left, half) in enumerate(zip(owns, lefts, chunks)):
        placed = [pltpu.with_memory_space_constraint(x, vmem) for x in (own, left)]
        extra = [] if image is None else [image]
        image = pl.pallas_call(
            functools.partial(render_kernel, sum(chunks[:c])),
            out_shape=jax.ShapeDtypeStruct((4, share, width), jnp.float32),
            in_specs=[pl.BlockSpec(memory_space=smem)] * 2
            + [pl.BlockSpec(memory_space=vmem)] * 3
            + [pl.BlockSpec(memory_space=pl.ANY)] * len(extra),
            out_specs=pl.BlockSpec(memory_space=pl.ANY),
            scratch_shapes=[
                pltpu.VMEM((layers, slabs, half, width), jnp.float32),
                pltpu.VMEM((4, half, width), jnp.float32),
                pltpu.SemaphoreType.DMA(()),
            ],
            input_output_aliases={5: 0} if extra else {},
        )(sheetgroup_viewer_sequence, skew_offsets, *placed, colormap_samples, *extra)
    return image


def solution(mesh):
    in_specs = (P("depth", None, "region"), P(), P(), P("depth", "region"), P())
    out_specs = P(None, "depth", "region")
    return jax.shard_map(shards, mesh=mesh, in_specs=in_specs, out_specs=out_specs, check_vma=False)
```

```python
import functools

import jax
import jax.numpy as jnp
from jax import lax
from jax.experimental import pallas as pl
from jax.experimental.pallas import tpu as pltpu
from jax.sharding import PartitionSpec as P

EMPTY = 1.0e6
LANES = 128
SUBLANES = 8


def partner(i, m, n, sign=1):
    if n & (n - 1) == 0:
        return i ^ m
    return (i + sign * m) % n


def slot_of(s, me, n):
    if n & (n - 1) == 0:
        return s ^ me
    return (s - me + n) % n


def lookup(cells, tables, knot_count):
    scaled = jnp.clip((cells + 3.0) * ((knot_count - 1) / 6.0), 0.0, knot_count - 1.0)
    lower = jnp.minimum(jnp.floor(scaled), knot_count - 2.0)
    fraction = scaled - lower
    index = lower.astype(jnp.int32)
    upper_half = index >= LANES
    lane = jnp.where(upper_half, index - LANES, index)
    values = []
    for c in range(4):
        picked = []
        for base in (0, 8):
            low = jnp.take_along_axis(tables[base + 2 * c], lane, axis=1, mode="promise_in_bounds")
            high = jnp.take_along_axis(tables[base + 2 * c + 1], lane, axis=1, mode="promise_in_bounds")
            picked.append(jnp.where(upper_half, high, low))
        values.append(picked[0] + fraction * picked[1])
    return values


def render_kernel(first_row, seq_ref, skew_ref, own_ref, left_ref, cmap_ref, *refs):
    out_hbm, shifted_ref, out_ref, sem = refs[-4:]
    halves = 1
    own_refs, left_refs = (own_ref,), (left_ref,)
    slabs, layers, half_rows, width = own_refs[0].shape
    rows = half_rows * halves
    layers_overall = layers * slabs
    knot_count = cmap_ref.shape[1]
    first_tile = lax.axis_index("region") == 0
    me = lax.axis_index("depth")
    skew = skew_ref[0]

    order = []
    for k in range(slabs):
        s = jnp.int32(0)
        for j in range(slabs):
            s = s + jnp.where(seq_ref[j] == k, j, 0)
        order.append(slot_of(s, me, slabs))

    for k in range(slabs):
        s = order[k]
        for l in range(layers):
            shift = ((k * layers + l) * skew) // layers_overall
            for r in range(rows // SUBLANES):
                band = pl.ds(r * SUBLANES, SUBLANES)
                c, rest = divmod(r * SUBLANES, half_rows)
                part = pl.ds(rest, SUBLANES)
                left = jnp.where(first_tile, EMPTY, left_refs[c][s, l, part, :])
                joined = jnp.concatenate([left, own_refs[c][s, l, part, :]], axis=1)
                shifted_ref[l, k, band, :] = pltpu.roll(joined, shift, 1)[:, width:]

    cmap = cmap_ref[...]
    following = pltpu.roll(cmap, knot_count - 1, 1)
    delta = following - cmap
    tables = []
    for src in (cmap, delta):
        for c in range(4):
            for h in range(knot_count // LANES):
                row = src[c : c + 1, h * LANES : (h + 1) * LANES]
                tables.append(jnp.broadcast_to(row, (SUBLANES, LANES)))

    pieces = width // LANES

    def block(i, carry):
        r = i // pieces
        j = i % pieces
        band = pl.ds(pl.multiple_of(r * SUBLANES, SUBLANES), SUBLANES)
        cols = pl.ds(pl.multiple_of(j * LANES, LANES), LANES)
        depth_sum = jnp.zeros((SUBLANES, LANES), jnp.float32)
        image = [jnp.zeros((SUBLANES, LANES), jnp.float32) for _ in range(3)]
        for k in range(slabs):
            tau = None
            color = None
            for l in range(layers):
                cells = shifted_ref[l, k, band, cols]
                values = lookup(cells, tables, knot_count)
                absorb = jnp.where(cells < 100.0, values[3] * (6.0 / layers_overall), 0.0)
                through = jnp.exp(-absorb)
                opacity = 1.0 - through
                emit = [values[c] * opacity for c in range(3)]
                if tau is None:
                    color = emit
                    tau = absorb
                else:
                    fade = jnp.exp(-tau)
                    color = [color[c] + fade * emit[c] for c in range(3)]
                    tau = tau + absorb
            if k == 0:
                image = color
            else:
                fade = jnp.exp(-depth_sum)
                image = [image[c] + fade * color[c] for c in range(3)]
            depth_sum = depth_sum + tau
        for c in range(3):
            out_ref[c, band, cols] = image[c]
        out_ref[3, band, cols] = 1.0 - jnp.exp(-depth_sum)
        return carry

    lax.fori_loop(0, (rows // SUBLANES) * pieces, block, 0)
    copy = pltpu.make_async_copy(out_ref, out_hbm.at[:, pl.ds(first_row, rows), :], sem)
    copy.start()
    copy.wait()


def shards(thermal_grid, colormap_samples, sheetgroup_viewer_sequence, occupied_lines, skew_offsets):
    layers, rows, width = thermal_grid.shape
    slabs = lax.axis_size("depth")
    regions = lax.axis_size("region")
    share = rows // slabs
    me = lax.axis_index("depth")
    halves = 2 if share % (2 * SUBLANES) == 0 else 1
    half = share // halves
    line = lax.broadcasted_iota(jnp.int32, (1, half, 1), 1)
    owns, lefts = [], []
    for c in range(halves):
        source = thermal_grid if c == 0 else lax.optimization_barrier(thermal_grid)
        held = []
        for m in range(slabs):
            start = partner(me, m, slabs, -1) * share + c * half
            piece = lax.dynamic_slice_in_dim(source, start, half, axis=1)
            piece = jnp.where(start + line < occupied_lines[0, 0], piece, EMPTY)
            if m > 0:
                route = [(i, partner(i, m, slabs, -1)) for i in range(slabs)]
                piece = lax.ppermute(piece, "depth", route)
            held.append(piece)
        own = jnp.stack(held, axis=0)
        owns.append(own)
        lefts.append(lax.ppermute(own, "region", [(i, i + 1) for i in range(regions - 1)]))
    vmem = pltpu.VMEM
    smem = pltpu.SMEM
    image = None
    for c, (own, left) in enumerate(zip(owns, lefts)):
        placed = [pltpu.with_memory_space_constraint(x, vmem) for x in (own, left)]
        extra = [] if image is None else [image]
        image = pl.pallas_call(
            functools.partial(render_kernel, c * half),
            out_shape=jax.ShapeDtypeStruct((4, share, width), jnp.float32),
            in_specs=[pl.BlockSpec(memory_space=smem)] * 2
            + [pl.BlockSpec(memory_space=vmem)] * 3
            + [pl.BlockSpec(memory_space=pl.ANY)] * len(extra),
            out_specs=pl.BlockSpec(memory_space=pl.ANY),
            scratch_shapes=[
                pltpu.VMEM((layers, slabs, half, width), jnp.float32),
                pltpu.VMEM((4, half, width), jnp.float32),
                pltpu.SemaphoreType.DMA(()),
            ],
            input_output_aliases={5: 0} if extra else {},
        )(sheetgroup_viewer_sequence, skew_offsets, *placed, colormap_samples, *extra)
    return image


def solution(mesh):
    in_specs = (P("depth", None, "region"), P(), P(), P("depth", "region"), P())
    out_specs = P(None, "depth", "region")
    return jax.shard_map(shards, mesh=mesh, in_specs=in_specs, out_specs=out_specs, check_vma=False)
```

```python
import functools

import jax
import jax.numpy as jnp
from jax import lax
from jax.experimental import pallas as pl
from jax.experimental.pallas import tpu as pltpu
from jax.sharding import PartitionSpec as P

EMPTY = 1.0e6
LANES = 128
SUBLANES = 8


def partner(i, m, n, sign=1):
    if n & (n - 1) == 0:
        return i ^ m
    return (i + sign * m) % n


def slot_of(s, me, n):
    if n & (n - 1) == 0:
        return s ^ me
    return (s - me + n) % n


def lookup(cells, tables, knot_count):
    scaled = jnp.clip((cells + 3.0) * ((knot_count - 1) / 6.0), 0.0, knot_count - 1.0)
    lower = jnp.minimum(jnp.floor(scaled), knot_count - 2.0)
    fraction = scaled - lower
    index = lower.astype(jnp.int32)
    upper_half = index >= LANES
    lane = jnp.where(upper_half, index - LANES, index)
    values = []
    for c in range(4):
        picked = []
        for base in (0, 8):
            low = jnp.take_along_axis(tables[base + 2 * c], lane, axis=1, mode="promise_in_bounds")
            high = jnp.take_along_axis(tables[base + 2 * c + 1], lane, axis=1, mode="promise_in_bounds")
            picked.append(jnp.where(upper_half, high, low))
        values.append(picked[0] + fraction * picked[1])
    return values


def render_kernel(first_row, seq_ref, skew_ref, own_ref, left_ref, cmap_ref, *refs):
    out_hbm, shifted_ref, out_ref, sem = refs[-4:]
    halves = 1
    own_refs, left_refs = (own_ref,), (left_ref,)
    slabs, layers, half_rows, width = own_refs[0].shape
    rows = half_rows * halves
    layers_overall = layers * slabs
    knot_count = cmap_ref.shape[1]
    first_tile = lax.axis_index("region") == 0
    me = lax.axis_index("depth")
    skew = skew_ref[0]

    order = []
    for k in range(slabs):
        s = jnp.int32(0)
        for j in range(slabs):
            s = s + jnp.where(seq_ref[j] == k, j, 0)
        order.append(slot_of(s, me, slabs))

    for k in range(slabs):
        s = order[k]
        for l in range(layers):
            shift = ((k * layers + l) * skew) // layers_overall
            for r in range(rows // SUBLANES):
                band = pl.ds(r * SUBLANES, SUBLANES)
                c, rest = divmod(r * SUBLANES, half_rows)
                part = pl.ds(rest, SUBLANES)
                left = jnp.where(first_tile, EMPTY, left_refs[c][s, l, part, :])
                joined = jnp.concatenate([left, own_refs[c][s, l, part, :]], axis=1)
                shifted_ref[l, k, band, :] = pltpu.roll(joined, shift, 1)[:, width:]

    cmap = cmap_ref[...]
    following = pltpu.roll(cmap, knot_count - 1, 1)
    delta = following - cmap
    tables = []
    for src in (cmap, delta):
        for c in range(4):
            for h in range(knot_count // LANES):
                row = src[c : c + 1, h * LANES : (h + 1) * LANES]
                tables.append(jnp.broadcast_to(row, (SUBLANES, LANES)))

    pieces = width // LANES

    def block(i, carry):
        r = i // pieces
        j = i % pieces
        band = pl.ds(pl.multiple_of(r * SUBLANES, SUBLANES), SUBLANES)
        cols = pl.ds(pl.multiple_of(j * LANES, LANES), LANES)
        depth_sum = jnp.zeros((SUBLANES, LANES), jnp.float32)
        image = [jnp.zeros((SUBLANES, LANES), jnp.float32) for _ in range(3)]
        for k in range(slabs):
            tau = None
            color = None
            for l in range(layers):
                cells = shifted_ref[l, k, band, cols]
                values = lookup(cells, tables, knot_count)
                absorb = jnp.where(cells < 100.0, values[3] * (6.0 / layers_overall), 0.0)
                through = jnp.exp(-absorb)
                opacity = 1.0 - through
                emit = [values[c] * opacity for c in range(3)]
                if tau is None:
                    color = emit
                    tau = absorb
                else:
                    fade = jnp.exp(-tau)
                    color = [color[c] + fade * emit[c] for c in range(3)]
                    tau = tau + absorb
            if k == 0:
                image = color
            else:
                fade = jnp.exp(-depth_sum)
                image = [image[c] + fade * color[c] for c in range(3)]
            depth_sum = depth_sum + tau
        for c in range(3):
            out_ref[c, band, cols] = image[c]
        out_ref[3, band, cols] = 1.0 - jnp.exp(-depth_sum)
        return carry

    lax.fori_loop(0, (rows // SUBLANES) * pieces, block, 0)
    copy = pltpu.make_async_copy(out_ref, out_hbm.at[:, pl.ds(first_row, rows), :], sem)
    copy.start()
    copy.wait()


def shards(thermal_grid, colormap_samples, sheetgroup_viewer_sequence, occupied_lines, skew_offsets):
    layers, rows, width = thermal_grid.shape
    slabs = lax.axis_size("depth")
    regions = lax.axis_size("region")
    share = rows // slabs
    me = lax.axis_index("depth")
    halves = 2 if share % (2 * SUBLANES) == 0 else 1
    half = share // halves
    line = lax.broadcasted_iota(jnp.int32, (1, half, 1), 1)
    owns, lefts = [], []
    near = None
    if halves > 1:
        first = partner(me, 1, slabs, -1) * share
        rows_all = lax.broadcasted_iota(jnp.int32, (1, share, 1), 1)
        near = lax.dynamic_slice_in_dim(thermal_grid, first, share, axis=1)
        near = jnp.where(first + rows_all < occupied_lines[0, 0], near, EMPTY)
        near = lax.ppermute(near, "depth", [(i, partner(i, 1, slabs, -1)) for i in range(slabs)])
    for c in range(halves):
        source = thermal_grid if c == 0 else lax.optimization_barrier(thermal_grid)
        held = []
        for m in range(slabs):
            start = partner(me, m, slabs, -1) * share + c * half
            piece = lax.dynamic_slice_in_dim(source, start, half, axis=1)
            piece = jnp.where(start + line < occupied_lines[0, 0], piece, EMPTY)
            if m == 1 and near is not None:
                piece = near[:, c * half : (c + 1) * half]
            elif m > 0:
                route = [(i, partner(i, m, slabs, -1)) for i in range(slabs)]
                piece = lax.ppermute(piece, "depth", route)
            held.append(piece)
        own = jnp.stack(held, axis=0)
        owns.append(own)
        lefts.append(lax.ppermute(own, "region", [(i, i + 1) for i in range(regions - 1)]))
    vmem = pltpu.VMEM
    smem = pltpu.SMEM
    image = None
    for c, (own, left) in enumerate(zip(owns, lefts)):
        placed = [pltpu.with_memory_space_constraint(x, vmem) for x in (own, left)]
        extra = [] if image is None else [image]
        image = pl.pallas_call(
            functools.partial(render_kernel, c * half),
            out_shape=jax.ShapeDtypeStruct((4, share, width), jnp.float32),
            in_specs=[pl.BlockSpec(memory_space=smem)] * 2
            + [pl.BlockSpec(memory_space=vmem)] * 3
            + [pl.BlockSpec(memory_space=pl.ANY)] * len(extra),
            out_specs=pl.BlockSpec(memory_space=pl.ANY),
            scratch_shapes=[
                pltpu.VMEM((layers, slabs, half, width), jnp.float32),
                pltpu.VMEM((4, half, width), jnp.float32),
                pltpu.SemaphoreType.DMA(()),
            ],
            input_output_aliases={5: 0} if extra else {},
        )(sheetgroup_viewer_sequence, skew_offsets, *placed, colormap_samples, *extra)
    return image


def solution(mesh):
    in_specs = (P("depth", None, "region"), P(), P(), P("depth", "region"), P())
    out_specs = P(None, "depth", "region")
    return jax.shard_map(shards, mesh=mesh, in_specs=in_specs, out_specs=out_specs, check_vma=False)
```

```python
import functools

import jax
import jax.numpy as jnp
from jax import lax
from jax.experimental import pallas as pl
from jax.experimental.pallas import tpu as pltpu
from jax.sharding import PartitionSpec as P

EMPTY = 1.0e6
LANES = 128
SUBLANES = 8


def partner(i, m, n, sign=1):
    if n & (n - 1) == 0:
        return i ^ m
    return (i + sign * m) % n


def slot_of(s, me, n):
    if n & (n - 1) == 0:
        return s ^ me
    return (s - me + n) % n


def left_widths(slabs, layers, width):
    widths = []
    for k in range(slabs):
        reach = ((k * layers + layers - 1) * (width - 1)) // (layers * slabs)
        widths.append(min(width, max(LANES, -(-reach // LANES) * LANES)))
    return widths


def lookup(cells, tables, knot_count):
    scaled = jnp.clip((cells + 3.0) * ((knot_count - 1) / 6.0), 0.0, knot_count - 1.0)
    lower = jnp.minimum(jnp.floor(scaled), knot_count - 2.0)
    fraction = scaled - lower
    index = lower.astype(jnp.int32)
    upper_half = index >= LANES
    lane = jnp.where(upper_half, index - LANES, index)
    values = []
    for c in range(4):
        picked = []
        for base in (0, 8):
            low = jnp.take_along_axis(tables[base + 2 * c], lane, axis=1, mode="promise_in_bounds")
            high = jnp.take_along_axis(tables[base + 2 * c + 1], lane, axis=1, mode="promise_in_bounds")
            picked.append(jnp.where(upper_half, high, low))
        values.append(picked[0] + fraction * picked[1])
    return values


def render_kernel(first_row, seq_ref, skew_ref, own_ref, left_ref, cmap_ref, *refs):
    out_hbm, shifted_ref, out_ref, sem = refs[-4:]
    halves = 1
    own_refs, left_refs = (own_ref,), (left_ref,)
    slabs, layers, half_rows, width = own_refs[0].shape
    widths = left_widths(slabs, layers, width)
    offsets = [sum(widths[:k]) for k in range(slabs)]
    rows = half_rows * halves
    layers_overall = layers * slabs
    knot_count = cmap_ref.shape[1]
    first_tile = lax.axis_index("region") == 0
    me = lax.axis_index("depth")
    skew = skew_ref[0]

    order = []
    for k in range(slabs):
        s = jnp.int32(0)
        for j in range(slabs):
            s = s + jnp.where(seq_ref[j] == k, j, 0)
        order.append(slot_of(s, me, slabs))

    for k in range(slabs):
        s = order[k]
        for l in range(layers):
            shift = ((k * layers + l) * skew) // layers_overall
            for r in range(rows // SUBLANES):
                band = pl.ds(r * SUBLANES, SUBLANES)
                c, rest = divmod(r * SUBLANES, half_rows)
                part = pl.ds(rest, SUBLANES)
                reach = widths[k]
                left = left_refs[c][l, part, pl.ds(offsets[k], reach)]
                left = jnp.where(first_tile, EMPTY, left)
                joined = jnp.concatenate([left, own_refs[c][s, l, part, :]], axis=1)
                shifted_ref[l, k, band, :] = pltpu.roll(joined, shift, 1)[:, reach:]

    cmap = cmap_ref[...]
    following = pltpu.roll(cmap, knot_count - 1, 1)
    delta = following - cmap
    tables = []
    for src in (cmap, delta):
        for c in range(4):
            for h in range(knot_count // LANES):
                row = src[c : c + 1, h * LANES : (h + 1) * LANES]
                tables.append(jnp.broadcast_to(row, (SUBLANES, LANES)))

    pieces = width // LANES

    def block(i, carry):
        r = i // pieces
        j = i % pieces
        band = pl.ds(pl.multiple_of(r * SUBLANES, SUBLANES), SUBLANES)
        cols = pl.ds(pl.multiple_of(j * LANES, LANES), LANES)
        depth_sum = jnp.zeros((SUBLANES, LANES), jnp.float32)
        image = [jnp.zeros((SUBLANES, LANES), jnp.float32) for _ in range(3)]
        for k in range(slabs):
            tau = None
            color = None
            for l in range(layers):
                cells = shifted_ref[l, k, band, cols]
                values = lookup(cells, tables, knot_count)
                absorb = jnp.where(cells < 100.0, values[3] * (6.0 / layers_overall), 0.0)
                through = jnp.exp(-absorb)
                opacity = 1.0 - through
                emit = [values[c] * opacity for c in range(3)]
                if tau is None:
                    color = emit
                    tau = absorb
                else:
                    fade = jnp.exp(-tau)
                    color = [color[c] + fade * emit[c] for c in range(3)]
                    tau = tau + absorb
            if k == 0:
                image = color
            else:
                fade = jnp.exp(-depth_sum)
                image = [image[c] + fade * color[c] for c in range(3)]
            depth_sum = depth_sum + tau
        for c in range(3):
            out_ref[c, band, cols] = image[c]
        out_ref[3, band, cols] = 1.0 - jnp.exp(-depth_sum)
        return carry

    lax.fori_loop(0, (rows // SUBLANES) * pieces, block, 0)
    copy = pltpu.make_async_copy(out_ref, out_hbm.at[:, pl.ds(first_row, rows), :], sem)
    copy.start()
    copy.wait()


def shards(thermal_grid, colormap_samples, sheetgroup_viewer_sequence, occupied_lines, skew_offsets):
    layers, rows, width = thermal_grid.shape
    slabs = lax.axis_size("depth")
    regions = lax.axis_size("region")
    share = rows // slabs
    me = lax.axis_index("depth")
    halves = 2 if share % (2 * SUBLANES) == 0 else 1
    half = share // halves
    line = lax.broadcasted_iota(jnp.int32, (1, half, 1), 1)
    widths = left_widths(slabs, layers, width)
    ranks = jnp.arange(slabs, dtype=jnp.int32)
    at_rank = sheetgroup_viewer_sequence[None, :] == ranks[:, None]
    slab_at_rank = jnp.sum(jnp.where(at_rank, ranks[None, :], 0), axis=1)
    rank_slots = [slot_of(slab_at_rank[k], me, slabs) for k in range(slabs)]
    owns, lefts = [], []
    for c in range(halves):
        source = thermal_grid if c == 0 else lax.optimization_barrier(thermal_grid)
        held = []
        for m in range(slabs):
            start = partner(me, m, slabs, -1) * share + c * half
            piece = lax.dynamic_slice_in_dim(source, start, half, axis=1)
            piece = jnp.where(start + line < occupied_lines[0, 0], piece, EMPTY)
            if m > 0:
                route = [(i, partner(i, m, slabs, -1)) for i in range(slabs)]
                piece = lax.ppermute(piece, "depth", route)
            held.append(piece)
        own = jnp.stack(held, axis=0)
        owns.append(own)
        reach = [
            lax.dynamic_index_in_dim(own, slot, axis=0, keepdims=False)[:, :, width - w :]
            for slot, w in zip(rank_slots, widths)
        ]
        trimmed = jnp.concatenate(reach, axis=2)
        lefts.append(lax.ppermute(trimmed, "region", [(i, i + 1) for i in range(regions - 1)]))
    vmem = pltpu.VMEM
    smem = pltpu.SMEM
    image = None
    for c, (own, left) in enumerate(zip(owns, lefts)):
        placed = [pltpu.with_memory_space_constraint(x, vmem) for x in (own, left)]
        extra = [] if image is None else [image]
        image = pl.pallas_call(
            functools.partial(render_kernel, c * half),
            out_shape=jax.ShapeDtypeStruct((4, share, width), jnp.float32),
            in_specs=[pl.BlockSpec(memory_space=smem)] * 2
            + [pl.BlockSpec(memory_space=vmem)] * 3
            + [pl.BlockSpec(memory_space=pl.ANY)] * len(extra),
            out_specs=pl.BlockSpec(memory_space=pl.ANY),
            scratch_shapes=[
                pltpu.VMEM((layers, slabs, half, width), jnp.float32),
                pltpu.VMEM((4, half, width), jnp.float32),
                pltpu.SemaphoreType.DMA(()),
            ],
            input_output_aliases={5: 0} if extra else {},
        )(sheetgroup_viewer_sequence, skew_offsets, *placed, colormap_samples, *extra)
    return image


def solution(mesh):
    in_specs = (P("depth", None, "region"), P(), P(), P("depth", "region"), P())
    out_specs = P(None, "depth", "region")
    return jax.shard_map(shards, mesh=mesh, in_specs=in_specs, out_specs=out_specs, check_vma=False)
```

```python
import functools

import jax
import jax.numpy as jnp
from jax import lax
from jax.experimental import pallas as pl
from jax.experimental.pallas import tpu as pltpu
from jax.sharding import PartitionSpec as P

EMPTY = 1.0e6
LANES = 128
SUBLANES = 8


def partner(i, m, n, sign=1):
    if n & (n - 1) == 0:
        return i ^ m
    return (i + sign * m) % n


def slot_of(s, me, n):
    if n & (n - 1) == 0:
        return s ^ me
    return (s - me + n) % n


def lookup(cells, tables, knot_count):
    scaled = jnp.clip((cells + 3.0) * ((knot_count - 1) / 6.0), 0.0, knot_count - 1.0)
    lower = jnp.minimum(jnp.floor(scaled), knot_count - 2.0)
    fraction = scaled - lower
    index = lower.astype(jnp.int32)
    upper_half = index >= LANES
    lane = jnp.where(upper_half, index - LANES, index)
    values = []
    for c in range(4):
        picked = []
        for base in (0, 8):
            low = jnp.take_along_axis(tables[base + 2 * c], lane, axis=1, mode="promise_in_bounds")
            high = jnp.take_along_axis(tables[base + 2 * c + 1], lane, axis=1, mode="promise_in_bounds")
            picked.append(jnp.where(upper_half, high, low))
        values.append(picked[0] + fraction * picked[1])
    return values


def tables_of(cmap_ref):
    knot_count = cmap_ref.shape[1]
    cmap = cmap_ref[...]
    following = pltpu.roll(cmap, knot_count - 1, 1)
    delta = following - cmap
    tables = []
    for src in (cmap, delta):
        for c in range(4):
            for h in range(knot_count // LANES):
                row = src[c : c + 1, h * LANES : (h + 1) * LANES]
                tables.append(jnp.broadcast_to(row, (SUBLANES, LANES)))
    return tables


def slots_by_rank(seq_ref, slabs):
    me = lax.axis_index("depth")
    order = []
    for k in range(slabs):
        s = jnp.int32(0)
        for j in range(slabs):
            s = s + jnp.where(seq_ref[j] == k, j, 0)
        order.append(slot_of(s, me, slabs))
    return order


def cell_terms(cells, tables, knot_count, layers_overall):
    values = lookup(cells, tables, knot_count)
    absorb = jnp.where(cells < 100.0, values[3] * (6.0 / layers_overall), 0.0)
    opacity = 1.0 - jnp.exp(-absorb)
    return [absorb] + [values[c] * opacity for c in range(3)]


def own_kernel(seq_ref, skew_ref, own_ref, cmap_ref, terms_ref, shifted_ref):
    slabs, layers, rows, width = own_ref.shape
    layers_overall = layers * slabs
    knot_count = cmap_ref.shape[1]
    skew = skew_ref[0]
    order = slots_by_rank(seq_ref, slabs)
    for k in range(slabs):
        for l in range(layers):
            shift = ((k * layers + l) * skew) // layers_overall
            for r in range(rows // SUBLANES):
                band = pl.ds(r * SUBLANES, SUBLANES)
                shifted_ref[l, k, band, :] = pltpu.roll(own_ref[order[k], l, band, :], shift, 1)
    tables = tables_of(cmap_ref)
    pieces = width // LANES

    def block(i, carry):
        band = pl.ds(pl.multiple_of((i // pieces) * SUBLANES, SUBLANES), SUBLANES)
        cols = pl.ds(pl.multiple_of((i % pieces) * LANES, LANES), LANES)
        for k in range(slabs):
            for l in range(layers):
                terms = cell_terms(shifted_ref[l, k, band, cols], tables, knot_count, layers_overall)
                for t in range(4):
                    terms_ref[k * layers + l, t, band, cols] = terms[t]
        return carry

    lax.fori_loop(0, (rows // SUBLANES) * pieces, block, 0)


def render_kernel(first_row, seq_ref, skew_ref, own_ref, left_ref, cmap_ref, terms_ref, *refs):
    out_hbm, shifted_ref, out_ref, sem = refs[-4:]
    slabs, layers, rows, width = own_ref.shape
    layers_overall = layers * slabs
    knot_count = cmap_ref.shape[1]
    first_tile = lax.axis_index("region") == 0
    skew = skew_ref[0]
    order = slots_by_rank(seq_ref, slabs)
    shifts = {}

    for k in range(slabs):
        s = order[k]
        for l in range(layers):
            shift = ((k * layers + l) * skew) // layers_overall
            shifts[k, l] = shift
            for r in range(rows // SUBLANES):
                band = pl.ds(r * SUBLANES, SUBLANES)
                left = jnp.where(first_tile, EMPTY, left_ref[s, l, band, :])
                joined = jnp.concatenate([left, own_ref[s, l, band, :]], axis=1)
                shifted_ref[l, k, band, :] = pltpu.roll(joined, shift, 1)[:, width:]

    tables = tables_of(cmap_ref)
    pieces = width // LANES

    def block(i, carry):
        j = i % pieces
        band = pl.ds(pl.multiple_of((i // pieces) * SUBLANES, SUBLANES), SUBLANES)
        cols = pl.ds(pl.multiple_of(j * LANES, LANES), LANES)
        depth_sum = None
        image = None
        for k in range(slabs):
            tau = None
            color = None
            for l in range(layers):
                terms = lax.cond(
                    j * LANES < shifts[k, l],
                    lambda: tuple(cell_terms(shifted_ref[l, k, band, cols], tables, knot_count, layers_overall)),
                    lambda: tuple(terms_ref[k * layers + l, t, band, cols] for t in range(4)),
                )
                absorb, emit = terms[0], terms[1:]
                if tau is None:
                    color = list(emit)
                    tau = absorb
                else:
                    fade = jnp.exp(-tau)
                    color = [color[c] + fade * emit[c] for c in range(3)]
                    tau = tau + absorb
            if k == 0:
                image = color
                depth_sum = tau
            else:
                fade = jnp.exp(-depth_sum)
                image = [image[c] + fade * color[c] for c in range(3)]
                depth_sum = depth_sum + tau
        for c in range(3):
            out_ref[c, band, cols] = image[c]
        out_ref[3, band, cols] = 1.0 - jnp.exp(-depth_sum)
        return carry

    lax.fori_loop(0, (rows // SUBLANES) * pieces, block, 0)
    copy = pltpu.make_async_copy(out_ref, out_hbm.at[:, pl.ds(first_row, rows), :], sem)
    copy.start()
    copy.wait()


def shards(thermal_grid, colormap_samples, sheetgroup_viewer_sequence, occupied_lines, skew_offsets):
    layers, rows, width = thermal_grid.shape
    slabs = lax.axis_size("depth")
    regions = lax.axis_size("region")
    share = rows // slabs
    me = lax.axis_index("depth")
    halves = 2 if share % (2 * SUBLANES) == 0 else 1
    half = share // halves
    line = lax.broadcasted_iota(jnp.int32, (1, half, 1), 1)
    owns, lefts = [], []
    for c in range(halves):
        source = thermal_grid if c == 0 else lax.optimization_barrier(thermal_grid)
        held = []
        for m in range(slabs):
            start = partner(me, m, slabs, -1) * share + c * half
            piece = lax.dynamic_slice_in_dim(source, start, half, axis=1)
            piece = jnp.where(start + line < occupied_lines[0, 0], piece, EMPTY)
            if m > 0:
                route = [(i, partner(i, m, slabs, -1)) for i in range(slabs)]
                piece = lax.ppermute(piece, "depth", route)
            held.append(piece)
        own = jnp.stack(held, axis=0)
        owns.append(own)
        lefts.append(lax.ppermute(own, "region", [(i, i + 1) for i in range(regions - 1)]))
    vmem = pltpu.VMEM
    smem = pltpu.SMEM
    image = None
    for c, (own, left) in enumerate(zip(owns, lefts)):
        own_placed = pltpu.with_memory_space_constraint(own, vmem)
        terms = pl.pallas_call(
            own_kernel,
            out_shape=jax.ShapeDtypeStruct((slabs * layers, 4, half, width), jnp.float32),
            in_specs=[pl.BlockSpec(memory_space=smem)] * 2 + [pl.BlockSpec(memory_space=vmem)] * 2,
            out_specs=pl.BlockSpec(memory_space=vmem),
            scratch_shapes=[pltpu.VMEM((layers, slabs, half, width), jnp.float32)],
        )(sheetgroup_viewer_sequence, skew_offsets, own_placed, colormap_samples)
        placed = [pltpu.with_memory_space_constraint(x, vmem) for x in (own, left)]
        terms = pltpu.with_memory_space_constraint(terms, vmem)
        extra = [] if image is None else [image]
        image = pl.pallas_call(
            functools.partial(render_kernel, c * half),
            out_shape=jax.ShapeDtypeStruct((4, share, width), jnp.float32),
            in_specs=[pl.BlockSpec(memory_space=smem)] * 2
            + [pl.BlockSpec(memory_space=vmem)] * 4
            + [pl.BlockSpec(memory_space=pl.ANY)] * len(extra),
            out_specs=pl.BlockSpec(memory_space=pl.ANY),
            scratch_shapes=[
                pltpu.VMEM((layers, slabs, half, width), jnp.float32),
                pltpu.VMEM((4, half, width), jnp.float32),
                pltpu.SemaphoreType.DMA(()),
            ],
            input_output_aliases={6: 0} if extra else {},
        )(sheetgroup_viewer_sequence, skew_offsets, *placed, colormap_samples, terms, *extra)
    return image


def solution(mesh):
    in_specs = (P("depth", None, "region"), P(), P(), P("depth", "region"), P())
    out_specs = P(None, "depth", "region")
    return jax.shard_map(shards, mesh=mesh, in_specs=in_specs, out_specs=out_specs, check_vma=False)
```

```python
import functools

import jax
import jax.numpy as jnp
from jax import lax
from jax.experimental import pallas as pl
from jax.experimental.pallas import tpu as pltpu
from jax.sharding import PartitionSpec as P

EMPTY = 1.0e6
LANES = 128
SUBLANES = 8


def partner(i, m, n, sign=1):
    if n & (n - 1) == 0:
        return i ^ m
    return (i + sign * m) % n


def slot_of(s, me, n):
    if n & (n - 1) == 0:
        return s ^ me
    return (s - me + n) % n


def lookup(cells, tables, knot_count):
    scaled = jnp.clip((cells + 3.0) * ((knot_count - 1) / 6.0), 0.0, knot_count - 1.0)
    lower = jnp.minimum(jnp.floor(scaled), knot_count - 2.0)
    fraction = scaled - lower
    index = lower.astype(jnp.int32)
    upper_half = index >= LANES
    lane = jnp.where(upper_half, index - LANES, index)
    values = []
    for c in range(4):
        picked = []
        for base in (0, 8):
            low = jnp.take_along_axis(tables[base + 2 * c], lane, axis=1, mode="promise_in_bounds")
            high = jnp.take_along_axis(tables[base + 2 * c + 1], lane, axis=1, mode="promise_in_bounds")
            picked.append(jnp.where(upper_half, high, low))
        values.append(picked[0] + fraction * picked[1])
    return values


def render_kernel(first_row, seq_ref, skew_ref, own_ref, left_ref, cmap_ref, *refs):
    out_hbm, shifted_ref, out_ref, sem = refs[-4:]
    halves = 1
    own_refs, left_refs = (own_ref,), (left_ref,)
    slabs, layers, half_rows, width = own_refs[0].shape
    rows = half_rows * halves
    layers_overall = layers * slabs
    knot_count = cmap_ref.shape[1]
    first_tile = lax.axis_index("region") == 0
    me = lax.axis_index("depth")
    skew = skew_ref[0]

    order = []
    for k in range(slabs):
        s = jnp.int32(0)
        for j in range(slabs):
            s = s + jnp.where(seq_ref[j] == k, j, 0)
        order.append(slot_of(s, me, slabs))

    for k in range(slabs):
        s = order[k]
        for l in range(layers):
            shift = ((k * layers + l) * skew) // layers_overall
            for r in range(rows // SUBLANES):
                band = pl.ds(r * SUBLANES, SUBLANES)
                c, rest = divmod(r * SUBLANES, half_rows)
                part = pl.ds(rest, SUBLANES)
                left = jnp.where(first_tile, EMPTY, left_refs[c][s, l, part, :])
                joined = jnp.concatenate([left, own_refs[c][s, l, part, :]], axis=1)
                shifted_ref[l, k, band, :] = pltpu.roll(joined, shift, 1)[:, width:]

    cmap = cmap_ref[...]
    following = pltpu.roll(cmap, knot_count - 1, 1)
    delta = following - cmap
    tables = []
    for src in (cmap, delta):
        for c in range(4):
            for h in range(knot_count // LANES):
                row = src[c : c + 1, h * LANES : (h + 1) * LANES]
                tables.append(jnp.broadcast_to(row, (SUBLANES, LANES)))

    pieces = width // LANES

    def block(i, carry):
        r = i // pieces
        j = i % pieces
        band = pl.ds(pl.multiple_of(r * SUBLANES, SUBLANES), SUBLANES)
        cols = pl.ds(pl.multiple_of(j * LANES, LANES), LANES)
        depth_sum = jnp.zeros((SUBLANES, LANES), jnp.float32)
        image = [jnp.zeros((SUBLANES, LANES), jnp.float32) for _ in range(3)]
        for k in range(slabs):
            tau = None
            color = None
            for l in range(layers):
                cells = shifted_ref[l, k, band, cols]
                values = lookup(cells, tables, knot_count)
                absorb = jnp.where(cells < 100.0, values[3] * (6.0 / layers_overall), 0.0)
                through = jnp.exp(-absorb)
                opacity = 1.0 - through
                emit = [values[c] * opacity for c in range(3)]
                if tau is None:
                    color = emit
                    tau = absorb
                else:
                    fade = jnp.exp(-tau)
                    color = [color[c] + fade * emit[c] for c in range(3)]
                    tau = tau + absorb
            if k == 0:
                image = color
            else:
                fade = jnp.exp(-depth_sum)
                image = [image[c] + fade * color[c] for c in range(3)]
            depth_sum = depth_sum + tau
        for c in range(3):
            out_ref[c, band, cols] = image[c]
        out_ref[3, band, cols] = 1.0 - jnp.exp(-depth_sum)
        return carry

    lax.fori_loop(0, (rows // SUBLANES) * pieces, block, 0, unroll=4)
    copy = pltpu.make_async_copy(out_ref, out_hbm.at[:, pl.ds(first_row, rows), :], sem)
    copy.start()
    copy.wait()


def shards(thermal_grid, colormap_samples, sheetgroup_viewer_sequence, occupied_lines, skew_offsets):
    layers, rows, width = thermal_grid.shape
    slabs = lax.axis_size("depth")
    regions = lax.axis_size("region")
    share = rows // slabs
    me = lax.axis_index("depth")
    halves = 2 if share % (2 * SUBLANES) == 0 else 1
    half = share // halves
    line = lax.broadcasted_iota(jnp.int32, (1, half, 1), 1)
    owns, lefts = [], []
    for c in range(halves):
        source = thermal_grid if c == 0 else lax.optimization_barrier(thermal_grid)
        held = []
        for m in range(slabs):
            start = partner(me, m, slabs, -1) * share + c * half
            piece = lax.dynamic_slice_in_dim(source, start, half, axis=1)
            piece = jnp.where(start + line < occupied_lines[0, 0], piece, EMPTY)
            if m > 0:
                route = [(i, partner(i, m, slabs, -1)) for i in range(slabs)]
                piece = lax.ppermute(piece, "depth", route)
            held.append(piece)
        own = jnp.stack(held, axis=0)
        owns.append(own)
        lefts.append(lax.ppermute(own, "region", [(i, i + 1) for i in range(regions - 1)]))
    vmem = pltpu.VMEM
    smem = pltpu.SMEM
    image = None
    for c, (own, left) in enumerate(zip(owns, lefts)):
        placed = [pltpu.with_memory_space_constraint(x, vmem) for x in (own, left)]
        extra = [] if image is None else [image]
        image = pl.pallas_call(
            functools.partial(render_kernel, c * half),
            out_shape=jax.ShapeDtypeStruct((4, share, width), jnp.float32),
            in_specs=[pl.BlockSpec(memory_space=smem)] * 2
            + [pl.BlockSpec(memory_space=vmem)] * 3
            + [pl.BlockSpec(memory_space=pl.ANY)] * len(extra),
            out_specs=pl.BlockSpec(memory_space=pl.ANY),
            scratch_shapes=[
                pltpu.VMEM((layers, slabs, half, width), jnp.float32),
                pltpu.VMEM((4, half, width), jnp.float32),
                pltpu.SemaphoreType.DMA(()),
            ],
            input_output_aliases={5: 0} if extra else {},
        )(sheetgroup_viewer_sequence, skew_offsets, *placed, colormap_samples, *extra)
    return image


def solution(mesh):
    in_specs = (P("depth", None, "region"), P(), P(), P("depth", "region"), P())
    out_specs = P(None, "depth", "region")
    return jax.shard_map(shards, mesh=mesh, in_specs=in_specs, out_specs=out_specs, check_vma=False)
```

```python
import functools

import jax
import jax.numpy as jnp
from jax import lax
from jax.experimental import pallas as pl
from jax.experimental.pallas import tpu as pltpu
from jax.sharding import PartitionSpec as P

EMPTY = 1.0e6
LANES = 128
SUBLANES = 8


def partner(i, m, n, sign=1):
    return (i + sign * m) % n


def slot_of(s, me, n):
    return (s - me + n) % n


def lookup(cells, tables, knot_count):
    scaled = jnp.clip((cells + 3.0) * ((knot_count - 1) / 6.0), 0.0, knot_count - 1.0)
    lower = jnp.minimum(jnp.floor(scaled), knot_count - 2.0)
    fraction = scaled - lower
    index = lower.astype(jnp.int32)
    upper_half = index >= LANES
    lane = jnp.where(upper_half, index - LANES, index)
    values = []
    for c in range(4):
        picked = []
        for base in (0, 8):
            low = jnp.take_along_axis(tables[base + 2 * c], lane, axis=1, mode="promise_in_bounds")
            high = jnp.take_along_axis(tables[base + 2 * c + 1], lane, axis=1, mode="promise_in_bounds")
            picked.append(jnp.where(upper_half, high, low))
        values.append(picked[0] + fraction * picked[1])
    return values


def render_kernel(first_row, seq_ref, skew_ref, own_ref, left_ref, cmap_ref, *refs):
    out_hbm, shifted_ref, out_ref, sem = refs[-4:]
    halves = 1
    own_refs, left_refs = (own_ref,), (left_ref,)
    slabs, layers, half_rows, width = own_refs[0].shape
    rows = half_rows * halves
    layers_overall = layers * slabs
    knot_count = cmap_ref.shape[1]
    first_tile = lax.axis_index("region") == 0
    me = lax.axis_index("depth")
    skew = skew_ref[0]

    order = []
    for k in range(slabs):
        s = jnp.int32(0)
        for j in range(slabs):
            s = s + jnp.where(seq_ref[j] == k, j, 0)
        order.append(slot_of(s, me, slabs))

    for k in range(slabs):
        s = order[k]
        for l in range(layers):
            shift = ((k * layers + l) * skew) // layers_overall
            for r in range(rows // SUBLANES):
                band = pl.ds(r * SUBLANES, SUBLANES)
                c, rest = divmod(r * SUBLANES, half_rows)
                part = pl.ds(rest, SUBLANES)
                left = jnp.where(first_tile, EMPTY, left_refs[c][s, l, part, :])
                joined = jnp.concatenate([left, own_refs[c][s, l, part, :]], axis=1)
                shifted_ref[l, k, band, :] = pltpu.roll(joined, shift, 1)[:, width:]

    cmap = cmap_ref[...]
    following = pltpu.roll(cmap, knot_count - 1, 1)
    delta = following - cmap
    tables = []
    for src in (cmap, delta):
        for c in range(4):
            for h in range(knot_count // LANES):
                row = src[c : c + 1, h * LANES : (h + 1) * LANES]
                tables.append(jnp.broadcast_to(row, (SUBLANES, LANES)))

    pieces = width // LANES

    def block(i, carry):
        r = i // pieces
        j = i % pieces
        band = pl.ds(pl.multiple_of(r * SUBLANES, SUBLANES), SUBLANES)
        cols = pl.ds(pl.multiple_of(j * LANES, LANES), LANES)
        depth_sum = jnp.zeros((SUBLANES, LANES), jnp.float32)
        image = [jnp.zeros((SUBLANES, LANES), jnp.float32) for _ in range(3)]
        for k in range(slabs):
            tau = None
            color = None
            for l in range(layers):
                cells = shifted_ref[l, k, band, cols]
                values = lookup(cells, tables, knot_count)
                absorb = jnp.where(cells < 100.0, values[3] * (6.0 / layers_overall), 0.0)
                through = jnp.exp(-absorb)
                opacity = 1.0 - through
                emit = [values[c] * opacity for c in range(3)]
                if tau is None:
                    color = emit
                    tau = absorb
                else:
                    fade = jnp.exp(-tau)
                    color = [color[c] + fade * emit[c] for c in range(3)]
                    tau = tau + absorb
            if k == 0:
                image = color
            else:
                fade = jnp.exp(-depth_sum)
                image = [image[c] + fade * color[c] for c in range(3)]
            depth_sum = depth_sum + tau
        for c in range(3):
            out_ref[c, band, cols] = image[c]
        out_ref[3, band, cols] = 1.0 - jnp.exp(-depth_sum)
        return carry

    lax.fori_loop(0, (rows // SUBLANES) * pieces, block, 0, unroll=4)
    copy = pltpu.make_async_copy(out_ref, out_hbm.at[:, pl.ds(first_row, rows), :], sem)
    copy.start()
    copy.wait()


def shards(thermal_grid, colormap_samples, sheetgroup_viewer_sequence, occupied_lines, skew_offsets):
    layers, rows, width = thermal_grid.shape
    slabs = lax.axis_size("depth")
    regions = lax.axis_size("region")
    share = rows // slabs
    me = lax.axis_index("depth")
    halves = 2 if share % (2 * SUBLANES) == 0 else 1
    half = share // halves
    line = lax.broadcasted_iota(jnp.int32, (1, half, 1), 1)
    owns, lefts = [], []
    for c in range(halves):
        source = thermal_grid if c == 0 else lax.optimization_barrier(thermal_grid)
        held = []
        for m in range(slabs):
            start = partner(me, m, slabs, -1) * share + c * half
            piece = lax.dynamic_slice_in_dim(source, start, half, axis=1)
            piece = jnp.where(start + line < occupied_lines[0, 0], piece, EMPTY)
            if m > 0:
                route = [(i, partner(i, m, slabs, -1)) for i in range(slabs)]
                piece = lax.ppermute(piece, "depth", route)
            held.append(piece)
        own = jnp.stack(held, axis=0)
        owns.append(own)
        lefts.append(lax.ppermute(own, "region", [(i, i + 1) for i in range(regions - 1)]))
    vmem = pltpu.VMEM
    smem = pltpu.SMEM
    image = None
    for c, (own, left) in enumerate(zip(owns, lefts)):
        placed = [pltpu.with_memory_space_constraint(x, vmem) for x in (own, left)]
        extra = [] if image is None else [image]
        image = pl.pallas_call(
            functools.partial(render_kernel, c * half),
            out_shape=jax.ShapeDtypeStruct((4, share, width), jnp.float32),
            in_specs=[pl.BlockSpec(memory_space=smem)] * 2
            + [pl.BlockSpec(memory_space=vmem)] * 3
            + [pl.BlockSpec(memory_space=pl.ANY)] * len(extra),
            out_specs=pl.BlockSpec(memory_space=pl.ANY),
            scratch_shapes=[
                pltpu.VMEM((layers, slabs, half, width), jnp.float32),
                pltpu.VMEM((4, half, width), jnp.float32),
                pltpu.SemaphoreType.DMA(()),
            ],
            input_output_aliases={5: 0} if extra else {},
        )(sheetgroup_viewer_sequence, skew_offsets, *placed, colormap_samples, *extra)
    return image


def solution(mesh):
    in_specs = (P("depth", None, "region"), P(), P(), P("depth", "region"), P())
    out_specs = P(None, "depth", "region")
    return jax.shard_map(shards, mesh=mesh, in_specs=in_specs, out_specs=out_specs, check_vma=False)
```
